512 devices in a mesh: blk: 64 (over y_lo, z, core), tp: 8 (over y_hi, x).
Axes of the slice: x: 4, y: 8 (y_hi: 2, y_lo: 4; y = y_hi * 4 + y_lo), z: 8, core: 2. Of those that a mesh axis runs over, the one named last changes fastest.
Arguments:
- embeds: bfloat16 [8192, 5120], P('blk', 'tp')
- given_embeds: bfloat16 [8192, 5120], P('blk', 'tp')
- accept: int32 [8192], P('blk'), may hold values 0 or 1
- lengths: int32 [64], P('blk'), may hold values from 4 to 4096, as said below
- block_keep: int32 [64, 64], P('blk'), may hold values from 0 to 1
- norm_gain: bfloat16 [5120], replicated, may hold values from 0.25 to 1.75
- w_query: bfloat16 [5120, 5120], P('blk', 'tp'), may hold values from -0.078125 to 0.078125
- b_query: bfloat16 [5120], P('tp'), may hold values from -4 to 4
- w_key: bfloat16 [5120, 1024], P('blk', 'tp'), may hold values from -0.078125 to 0.078125
- b_key: bfloat16 [1024], P('tp'), may hold values from -4 to 4
- w_value: bfloat16 [5120, 1024], P('blk', 'tp'), may hold values from -0.078125 to 0.078125
- b_value: bfloat16 [1024], P('tp'), may hold values from -4 to 4
- cache_keys: bfloat16 [4096, 1024], P('blk', 'tp'), as said below
- cache_values: bfloat16 [4096, 1024], P('blk', 'tp'), may hold values from -6 to 6
Outputs:
- first_pass: bfloat16 [8192, 5120], P('blk', 'tp')
- second_pass: bfloat16 [8192, 5120], P('blk', 'tp')
The draws below stay inside these ranges and needn't reach their ends.
Inputs may be any that keep to these rules, and one draw needn't show every extreme that they name: `lengths`: every request sees at least the first 4 prompt positions; some request sees all 4096. `cache_keys`: entries lie between -160 and 160.
All inputs are finite; a program needn't handle non-finite values. No bound on the sum of `accept` on one device may be relied on, other than what follows from the above.
Results may differ from the reference program's by a relative error of at most 0.012.
The reference program's roundings to bfloat16 on the way count: a program that leaves them out, or rounds other values in their place, can miss the bound.
Values may be sent and summed in bfloat16 or wider, within the bound.
No kernel may reach another device: no remote copies, remote signals or barrier semaphores. Data moves between devices by JAX's collectives and lax.ppermute only.
A program may use at most 64 MiB of HBM per device.

```python
import math
import jax
import jax.numpy as jnp
from jax import lax

D = 5120
KVH = 8
HD = 128
HQ = 40
BL = 128
CB = 64
GQ = 5
REQ = 64
BLOCKS = 64
CTX = 4096
TOKENS = 8192


def scaled_rows(base_key, row_count, col_count):
    first_key, second_key, third_key = jax.random.split(base_key, 3)
    row_scale = jnp.exp(jax.random.uniform(first_key, (row_count, 1), jnp.float32, 0.0, math.log(10.0)))
    col_scale = jnp.exp(jax.random.uniform(second_key, (1, col_count), jnp.float32, 0.0, math.log(10.0)))
    base = jax.random.normal(third_key, (row_count, col_count), jnp.float32)
    return base * row_scale * col_scale


def draw_embeds(key, part):
    return scaled_rows(jax.random.fold_in(key, 11), TOKENS, D).astype(jnp.bfloat16)


def draw_given_embeds(key, part):
    return scaled_rows(jax.random.fold_in(key, 12), TOKENS, D).astype(jnp.bfloat16)


def draw_cache_keys(key, part):
    first_key = jax.random.fold_in(jax.random.fold_in(key, 21), 0)
    base = jnp.clip(jax.random.normal(first_key, (CTX, KVH * HD), jnp.float32) * 1.5, -9.0, 9.0)
    return base.astype(jnp.bfloat16)


def draw_lengths(key, part):
    first_key, second_key = jax.random.split(jax.random.fold_in(key, 31))
    drawn = jax.random.randint(first_key, (REQ,), 4, CTX + 1)
    chosen = jax.random.randint(second_key, (), 0, REQ)
    return jnp.where(jnp.arange(REQ, dtype=jnp.int32) == chosen, CTX, drawn).astype(jnp.int32)


def draw_block_keep(key, part):
    drawn = (jax.random.randint(jax.random.fold_in(key, 41), (REQ, BLOCKS), 0, 4) > 0).astype(jnp.int32)
    column_ids = jnp.arange(BLOCKS, dtype=jnp.int32)
    return jnp.where(column_ids[None, :] == 0, 1, drawn).astype(jnp.int32)


def place_ends(array, key, least, largest):
    longest = array.shape.index(max(array.shape))
    spots = []
    for shift in (0, 1):
        where = [jax.random.randint(jax.random.fold_in(key, axis), (), 0, length) for axis, length in enumerate(array.shape)]
        where[longest] = (where[longest] + shift) % array.shape[longest]
        spots.append(tuple(where))
    return array.at[spots[0]].set(least).at[spots[1]].set(largest)


def level_of(key, dims, cuts, smallest, largest):
    def one(position, parts):
        steps = jax.random.uniform(jax.random.fold_in(jax.random.fold_in(key, 6), position), (parts,), jnp.float32, smallest / len(cuts), largest / len(cuts))
        return jnp.repeat(jnp.exp(steps), dims[position] // parts).reshape((-1,) + (1,) * (len(dims) - position - 1))

    loudness = one(*cuts[0])
    for cut in cuts[1:]:
        loudness = loudness * one(*cut)
    return loudness


def centred(rng, shape, deviation, reach, shards=(), held_as=jnp.bfloat16):
    result = deviation * jax.random.normal(rng, shape, jnp.float32)
    if shards:
        result = result * level_of(rng, shape, shards, -0.22, 0.18)
    return jnp.clip(result, -reach, reach).astype(held_as)


def setup_inputs(seed: int = 0) -> dict:
    key_of = jax.random.split(jax.random.key(seed), 15)
    return {
        "embeds": draw_embeds(jax.random.fold_in(key_of[14], 71), 0),
        "given_embeds": draw_given_embeds(jax.random.fold_in(key_of[14], 71), 0),
        "accept": place_ends((jax.random.randint(key_of[2], (TOKENS,), 0, 2) < 1).astype(jnp.int32), jax.random.fold_in(key_of[2], 1), 0, 1),
        "lengths": draw_lengths(jax.random.fold_in(key_of[14], 71), 0),
        "block_keep": draw_block_keep(jax.random.fold_in(key_of[14], 71), 0),
        "norm_gain": jnp.clip(1.0 + 0.15 * jax.random.normal(key_of[5], (D,), jnp.float32), 0.25, 1.75).astype(jnp.bfloat16),
        "w_query": centred(key_of[6], (D, HQ * HD), D ** -0.5, 0.078125, ((0, 64), (1, 8))),
        "b_query": centred(key_of[7], (HQ * HD,), 1.0, 4.0, ((0, 8),)),
        "w_key": centred(key_of[8], (D, KVH * HD), D ** -0.5, 0.078125, ((0, 64), (1, 8))),
        "b_key": centred(key_of[9], (KVH * HD,), 1.0, 4.0, ((0, 8),)),
        "w_value": centred(key_of[10], (D, KVH * HD), D ** -0.5, 0.078125, ((0, 64), (1, 8))),
        "b_value": centred(key_of[11], (KVH * HD,), 1.0, 4.0, ((0, 8),)),
        "cache_keys": draw_cache_keys(jax.random.fold_in(key_of[14], 71), 0),
        "cache_values": centred(key_of[13], (CTX, KVH * HD), 1.0, 6.0, ((0, 64), (1, 8))),
    }


def rotate(vectors, positions):
    halfway = HD // 2
    frequency = 1000000.0 ** (-(jnp.arange(halfway, dtype=jnp.float32) * (2.0 / HD)))
    angles = positions[..., None] * frequency
    cosine = jnp.cos(angles)[..., None, :]
    sine_part = jnp.sin(angles)[..., None, :]
    front_part = vectors[..., :halfway]
    back_part = vectors[..., halfway:]
    return jnp.concatenate([front_part * cosine - back_part * sine_part, back_part * cosine + front_part * sine_part], axis=-1)

def normalize(rows_in, norm_gain):
    widened = rows_in.astype(jnp.float32)
    inverse = lax.rsqrt(lax.optimization_barrier(jnp.mean(widened * widened, axis=-1, keepdims=True)) + 1e-06)
    return (widened * inverse * norm_gain.astype(jnp.float32)).astype(jnp.bfloat16)

def reference(embeds, given_embeds, accept, lengths, block_keep, norm_gain, w_query, b_query, w_key, b_key, w_value, b_value, cache_keys, cache_values):
    revised = jnp.where(accept[:, None] == 1, given_embeds, embeds)
    normed = normalize(jnp.concatenate([embeds, revised], axis=0), norm_gain)
    queries = jnp.dot(normed, w_query, preferred_element_type=jnp.float32) + b_query.astype(jnp.float32)
    key_proj = jnp.dot(normed, w_key, preferred_element_type=jnp.float32) + b_key.astype(jnp.float32)
    value_proj = jnp.dot(normed, w_value, preferred_element_type=jnp.float32) + b_value.astype(jnp.float32)
    offsets = jnp.arange(BL, dtype=jnp.float32)
    positions = (lengths.astype(jnp.float32)[:, None] + offsets[None, :])[None]
    q_rot = rotate(queries.reshape(2, REQ, BL, HQ, HD), positions).astype(jnp.bfloat16)
    k_rot = rotate(key_proj.reshape(2, REQ, BL, KVH, HD), positions).astype(jnp.bfloat16)
    value_rows = value_proj.astype(jnp.bfloat16).reshape(2, REQ, BL, KVH, HD)
    q_rot = jnp.transpose(q_rot, (1, 0, 2, 3, 4))
    k_rot = jnp.transpose(k_rot, (1, 0, 2, 3, 4))
    value_rows = jnp.transpose(value_rows, (1, 0, 2, 3, 4))
    cache_k = cache_keys.reshape(CTX, KVH, HD).astype(jnp.float32)
    cache_v = cache_values.reshape(CTX, KVH, HD).astype(jnp.float32)
    cache_index = jnp.arange(CTX, dtype=jnp.int32)
    block_index = cache_index // CB
    inv_root = 1.0 / math.sqrt(HD)

    def per_request(request):
        q_req, k_req, v_req, length, keep_row = request
        q_float = q_req.astype(jnp.float32).reshape(2, BL, KVH, GQ, HD)
        own_scores = jnp.einsum('pqkgd,pjkd->pkgqj', q_float, k_req.astype(jnp.float32)) * inv_root
        far_scores = jnp.einsum('pqkgd,ckd->pkgqc', q_float, cache_k) * inv_root
        visible = (cache_index < length) & (keep_row[block_index] == 1)
        far_scores = jnp.where(visible, far_scores, -jnp.inf)
        highest = jnp.maximum(lax.optimization_barrier(jnp.max(own_scores, axis=-1)), lax.optimization_barrier(jnp.max(far_scores, axis=-1)))[..., None]
        own_weights = jnp.exp(own_scores - highest)
        far_weights = jnp.where(visible, jnp.exp(far_scores - highest), 0.0)
        totals = lax.optimization_barrier(jnp.sum(own_weights, axis=-1)) + lax.optimization_barrier(jnp.sum(far_weights, axis=-1))
        own_b = lax.optimization_barrier(own_weights.astype(jnp.bfloat16)).astype(jnp.float32)
        far_b = lax.optimization_barrier(far_weights.astype(jnp.bfloat16)).astype(jnp.float32)
        mixture = jnp.einsum('pkgqj,pjkd->pkgqd', own_b, v_req.astype(jnp.float32))
        mixture = mixture + jnp.einsum('pkgqc,ckd->pkgqd', far_b, cache_v)
        attended = mixture / totals[..., None]
        attended = jnp.transpose(attended, (0, 3, 1, 2, 4)).reshape(2, BL, HQ * HD)
        return attended.astype(jnp.bfloat16)
    attended = lax.map(per_request, (q_rot, k_rot, value_rows, lengths, block_keep))
    attended = jnp.transpose(attended, (1, 0, 2, 3)).reshape(2 * TOKENS, HQ * HD)
    return (attended[:TOKENS], attended[TOKENS:])
```

```python
import math

import jax
import jax.numpy as jnp
from jax import lax
from jax.experimental import pallas as pl
from jax.experimental.pallas import tpu as pltpu
from jax.sharding import PartitionSpec as P

KVH = 8
HD = 128
HQ = 40
CB = 64


def rotate(vectors, positions):
    halfway = HD // 2
    frequency = 1000000.0 ** (-(jnp.arange(halfway, dtype=jnp.float32) * (2.0 / HD)))
    angles = positions[..., None] * frequency
    cosine = jnp.cos(angles)[..., None, :]
    sine_part = jnp.sin(angles)[..., None, :]
    front_part = vectors[..., :halfway]
    back_part = vectors[..., halfway:]
    return jnp.concatenate(
        [front_part * cosine - back_part * sine_part, back_part * cosine + front_part * sine_part],
        axis=-1,
    )


def normalize(rows_in, norm_gain):
    widened = rows_in.astype(jnp.float32)
    inverse = lax.rsqrt(jnp.mean(widened * widened, axis=-1, keepdims=True) + 1e-06)
    return (widened * inverse * norm_gain.astype(jnp.float32)).astype(jnp.bfloat16)


def attend_kernel(q_ref, ko_ref, vo_ref, kc_ref, vc_ref, bias_ref, out_ref):
    inv_root = 1.0 / math.sqrt(HD)
    q = q_ref[...]
    contract = (((1,), (1,)), ((), ()))
    own = lax.dot_general(q, ko_ref[...], contract, preferred_element_type=jnp.float32) * inv_root
    far = lax.dot_general(q, kc_ref[...], contract, preferred_element_type=jnp.float32) * inv_root
    far = far + bias_ref[...]
    highest = jnp.maximum(jnp.max(own, axis=-1, keepdims=True), jnp.max(far, axis=-1, keepdims=True))
    own_w = jnp.exp(own - highest)
    far_w = jnp.exp(far - highest)
    totals = jnp.sum(own_w, axis=-1, keepdims=True) + jnp.sum(far_w, axis=-1, keepdims=True)
    mixture = jnp.dot(own_w.astype(jnp.bfloat16), vo_ref[...], preferred_element_type=jnp.float32)
    mixture = mixture + jnp.dot(far_w.astype(jnp.bfloat16), vc_ref[...], preferred_element_type=jnp.float32)
    out_ref[...] = (mixture / totals).astype(out_ref.dtype)


def attend(q_rot, k_rot, value_rows, cache_k, cache_v, bias):
    passes, rows, width = q_rot.shape
    heads = width // HD
    ctx = cache_k.shape[0]
    return pl.pallas_call(
        attend_kernel,
        grid=(passes, heads),
        in_specs=[
            pl.BlockSpec((None, rows, HD), lambda p, h: (p, 0, h)),
            pl.BlockSpec((None, rows, HD), lambda p, h: (p, 0, 0)),
            pl.BlockSpec((None, rows, HD), lambda p, h: (p, 0, 0)),
            pl.BlockSpec((ctx, HD), lambda p, h: (0, 0)),
            pl.BlockSpec((ctx, HD), lambda p, h: (0, 0)),
            pl.BlockSpec((1, ctx), lambda p, h: (0, 0)),
        ],
        out_specs=pl.BlockSpec((None, rows, HD), lambda p, h: (p, 0, h)),
        out_shape=jax.ShapeDtypeStruct((passes, rows, width), jnp.bfloat16),
        cost_estimate=pl.CostEstimate(
            flops=4 * passes * heads * rows * (ctx + rows) * HD,
            transcendentals=passes * heads * rows * (ctx + rows),
            bytes_accessed=2 * (2 * ctx * HD + 4 * passes * rows * width),
        ),
    )(q_rot, k_rot, value_rows, cache_k, cache_v, bias)


def local(
    embeds,
    given_embeds,
    accept,
    lengths,
    block_keep,
    norm_gain,
    w_query,
    b_query,
    w_key,
    b_key,
    w_value,
    b_value,
    cache_keys,
    cache_values,
):
    local_kv = w_key.shape[1] // HD
    block_rows = embeds.shape[0]
    ctx_rows = cache_keys.shape[0]
    q_cols = w_query.shape[1]
    w_rows = w_query.shape[0]

    both = lax.all_gather(jnp.stack([embeds, given_embeds]), "tp", axis=2, tiled=True)
    first_rows, given_rows = both[0], both[1]

    w_piece = jnp.concatenate([w_query, w_key, w_value], axis=1)
    c_piece = jnp.concatenate([cache_keys, cache_values], axis=1)
    w_size = w_piece.size
    packed = jnp.concatenate([w_piece.reshape(-1), c_piece.reshape(-1)])
    gathered = lax.all_gather(packed, "blk", axis=0, tiled=False)
    shards = gathered.shape[0]
    w_all = gathered[:, :w_size].reshape(shards * w_rows, w_piece.shape[1])
    c_all = gathered[:, w_size:].reshape(shards * ctx_rows, c_piece.shape[1])
    cache_k = c_all[:, : local_kv * HD]
    cache_v = c_all[:, local_kv * HD :]

    revised = jnp.where(accept[:, None] == 1, given_rows, first_rows)
    normed = normalize(jnp.concatenate([first_rows, revised], axis=0), norm_gain)
    proj = jnp.dot(normed, w_all, preferred_element_type=jnp.float32)
    queries = proj[:, :q_cols] + b_query.astype(jnp.float32)
    key_proj = proj[:, q_cols : q_cols + local_kv * HD] + b_key.astype(jnp.float32)
    value_proj = proj[:, q_cols + local_kv * HD :] + b_value.astype(jnp.float32)

    length = lengths[0]
    keep_row = block_keep[0]
    positions = length.astype(jnp.float32) + jnp.arange(block_rows, dtype=jnp.float32)
    q_rot = rotate(queries.reshape(2, block_rows, q_cols // HD, HD), positions).astype(jnp.bfloat16)
    k_rot = rotate(key_proj.reshape(2, block_rows, local_kv, HD), positions).astype(jnp.bfloat16)
    value_rows = value_proj.astype(jnp.bfloat16)

    total_ctx = shards * ctx_rows
    cache_index = jnp.arange(total_ctx, dtype=jnp.int32)
    visible = (cache_index < length) & (jnp.repeat(keep_row, CB, total_repeat_length=total_ctx) == 1)
    bias = jnp.where(visible, 0.0, -jnp.inf).astype(jnp.float32).reshape(1, total_ctx)

    attended = attend(
        q_rot.reshape(2, block_rows, q_cols),
        k_rot.reshape(2, block_rows, local_kv * HD),
        value_rows.reshape(2, block_rows, local_kv * HD),
        cache_k,
        cache_v,
        bias,
    )
    return (attended[0], attended[1])


def solution(mesh):
    return jax.shard_map(
        local,
        mesh=mesh,
        in_specs=(
            P("blk", "tp"),
            P("blk", "tp"),
            P("blk"),
            P("blk"),
            P("blk", None),
            P(),
            P("blk", "tp"),
            P("tp"),
            P("blk", "tp"),
            P("tp"),
            P("blk", "tp"),
            P("tp"),
            P("blk", "tp"),
            P("blk", "tp"),
        ),
        out_specs=(P("blk", "tp"), P("blk", "tp")),
        check_vma=False,
    )
```

```python
import math

import jax
import jax.numpy as jnp
from jax import lax
from jax.experimental import pallas as pl
from jax.experimental.pallas import tpu as pltpu
from jax.sharding import PartitionSpec as P

KVH = 8
HD = 128
HQ = 40
CB = 64


def rotate(vectors, positions):
    halfway = HD // 2
    frequency = 1000000.0 ** (-(jnp.arange(halfway, dtype=jnp.float32) * (2.0 / HD)))
    angles = positions[..., None] * frequency
    cosine = jnp.cos(angles)[..., None, :]
    sine_part = jnp.sin(angles)[..., None, :]
    front_part = vectors[..., :halfway]
    back_part = vectors[..., halfway:]
    return jnp.concatenate(
        [front_part * cosine - back_part * sine_part, back_part * cosine + front_part * sine_part],
        axis=-1,
    )


def normalize(rows_in, norm_gain):
    widened = rows_in.astype(jnp.float32)
    inverse = lax.rsqrt(jnp.mean(widened * widened, axis=-1, keepdims=True) + 1e-06)
    return (widened * inverse * norm_gain.astype(jnp.float32)).astype(jnp.bfloat16)


def attend_kernel(q_ref, ko_ref, vo_ref, kc_ref, vc_ref, bias_ref, out_ref):
    inv_root = 1.0 / math.sqrt(HD)
    q = q_ref[...]
    shards, ctx_rows, width = kc_ref.shape
    cache_k = kc_ref[...].reshape(shards * ctx_rows, width)
    cache_v = vc_ref[...].reshape(shards * ctx_rows, width)
    contract = (((1,), (1,)), ((), ()))
    own = lax.dot_general(q, ko_ref[...], contract, preferred_element_type=jnp.float32) * inv_root
    far = lax.dot_general(q, cache_k, contract, preferred_element_type=jnp.float32) * inv_root
    far = far + bias_ref[...]
    highest = jnp.maximum(jnp.max(own, axis=-1, keepdims=True), jnp.max(far, axis=-1, keepdims=True))
    own_w = jnp.exp(own - highest)
    far_w = jnp.exp(far - highest)
    totals = jnp.sum(own_w, axis=-1, keepdims=True) + jnp.sum(far_w, axis=-1, keepdims=True)
    mixture = jnp.dot(own_w.astype(jnp.bfloat16), vo_ref[...], preferred_element_type=jnp.float32)
    mixture = mixture + jnp.dot(far_w.astype(jnp.bfloat16), cache_v, preferred_element_type=jnp.float32)
    out_ref[...] = (mixture / totals).astype(out_ref.dtype)


def attend(q_rot, k_rot, value_rows, gathered, bias):
    passes, rows, width = q_rot.shape
    heads = width // HD
    shards, ignored, lanes = gathered.shape
    ctx = bias.shape[1]
    ctx_rows = ctx // shards
    return pl.pallas_call(
        attend_kernel,
        grid=(passes, heads),
        in_specs=[
            pl.BlockSpec((None, rows, HD), lambda p, h: (p, 0, h)),
            pl.BlockSpec((None, rows, HD), lambda p, h: (p, 0, 0)),
            pl.BlockSpec((None, rows, HD), lambda p, h: (p, 0, 0)),
            pl.BlockSpec((shards, ctx_rows, lanes), lambda p, h: (0, 0, 0)),
            pl.BlockSpec((shards, ctx_rows, lanes), lambda p, h: (0, 1, 0)),
            pl.BlockSpec((1, ctx), lambda p, h: (0, 0)),
        ],
        out_specs=pl.BlockSpec((None, rows, HD), lambda p, h: (p, 0, h)),
        out_shape=jax.ShapeDtypeStruct((passes, rows, width), jnp.bfloat16),
        cost_estimate=pl.CostEstimate(
            flops=4 * passes * heads * rows * (ctx + rows) * HD,
            transcendentals=passes * heads * rows * (ctx + rows),
            bytes_accessed=2 * (2 * ctx * HD + 4 * passes * rows * width),
        ),
    )(q_rot, k_rot, value_rows, gathered, gathered, bias)


def local(
    embeds,
    given_embeds,
    accept,
    lengths,
    block_keep,
    norm_gain,
    w_query,
    b_query,
    w_key,
    b_key,
    w_value,
    b_value,
    cache_keys,
    cache_values,
):
    local_kv = w_key.shape[1] // HD
    block_rows = embeds.shape[0]
    ctx_rows = cache_keys.shape[0]
    q_cols = w_query.shape[1]
    w_rows = w_query.shape[0]

    tp_size = lax.axis_size("tp")
    me_tp = lax.axis_index("tp")
    mine = jnp.stack([embeds, given_embeds])
    pieces = [mine]
    for shift in range(1, tp_size):
        pairs = [(i, (i - shift) % tp_size) for i in range(tp_size)]
        pieces.append(lax.ppermute(mine, "tp", pairs))
    ordered = jnp.roll(jnp.stack(pieces), me_tp, axis=0)
    both = jnp.concatenate([ordered[i] for i in range(tp_size)], axis=-1)
    first_rows, given_rows = both[0], both[1]

    w_cols = w_query.shape[1] // HD + 2 * local_kv
    w_parts = [w_query[:, j * HD : (j + 1) * HD] for j in range(q_cols // HD)] + [w_key, w_value]
    packed = jnp.concatenate([cache_keys, cache_values] + w_parts, axis=0)
    gathered = lax.all_gather(packed, "blk", axis=0, tiled=False)
    shards = gathered.shape[0]
    cache_rows = 2 * ctx_rows
    w_blocks = gathered[:, cache_rows:, :].reshape(shards, w_cols, w_rows, HD)
    revised = jnp.where(accept[:, None] == 1, given_rows, first_rows)
    normed = normalize(jnp.concatenate([first_rows, revised], axis=0), norm_gain)
    proj = jnp.einsum(
        "rsi,sjic->rjc",
        normed.reshape(normed.shape[0], shards, w_rows),
        w_blocks,
        preferred_element_type=jnp.float32,
    )
    queries = proj[:, : q_cols // HD, :].reshape(-1, q_cols) + b_query.astype(jnp.float32)
    key_proj = proj[:, q_cols // HD, :] + b_key.astype(jnp.float32)
    value_proj = proj[:, q_cols // HD + 1, :] + b_value.astype(jnp.float32)
    length = lengths[0]
    keep_row = block_keep[0]
    positions = length.astype(jnp.float32) + jnp.arange(block_rows, dtype=jnp.float32)
    q_rot = rotate(queries.reshape(2, block_rows, q_cols // HD, HD), positions).astype(jnp.bfloat16)
    k_rot = rotate(key_proj.reshape(2, block_rows, local_kv, HD), positions).astype(jnp.bfloat16)
    value_rows = value_proj.astype(jnp.bfloat16)

    total_ctx = shards * ctx_rows
    cache_index = jnp.arange(total_ctx, dtype=jnp.int32).reshape(-1, CB)
    kept = jnp.broadcast_to(keep_row.reshape(-1, 1), cache_index.shape) == 1
    visible = (cache_index < length) & kept
    bias = jnp.where(visible, 0.0, -jnp.inf).astype(jnp.float32).reshape(1, total_ctx)
    attended = attend(
        q_rot.reshape(2, block_rows, q_cols),
        k_rot.reshape(2, block_rows, local_kv * HD),
        value_rows.reshape(2, block_rows, local_kv * HD),
        gathered,
        bias,
    )
    return (attended[0], attended[1])


def solution(mesh):
    return jax.shard_map(
        local,
        mesh=mesh,
        in_specs=(
            P("blk", "tp"),
            P("blk", "tp"),
            P("blk"),
            P("blk"),
            P("blk", None),
            P(),
            P("blk", "tp"),
            P("tp"),
            P("blk", "tp"),
            P("tp"),
            P("blk", "tp"),
            P("tp"),
            P("blk", "tp"),
            P("blk", "tp"),
        ),
        out_specs=(P("blk", "tp"), P("blk", "tp")),
        check_vma=False,
    )
```

```python
import math

import jax
import jax.numpy as jnp
from jax import lax
from jax.experimental import pallas as pl
from jax.experimental.pallas import tpu as pltpu
from jax.sharding import Mesh
from jax.sharding import PartitionSpec as P

KVH = 8
HD = 128
HQ = 40
CB = 64


def rotate(vectors, positions):
    halfway = HD // 2
    frequency = 1000000.0 ** (-(jnp.arange(halfway, dtype=jnp.float32) * (2.0 / HD)))
    angles = positions[..., None] * frequency
    cosine = jnp.cos(angles)[..., None, :]
    sine_part = jnp.sin(angles)[..., None, :]
    front_part = vectors[..., :halfway]
    back_part = vectors[..., halfway:]
    return jnp.concatenate(
        [front_part * cosine - back_part * sine_part, back_part * cosine + front_part * sine_part],
        axis=-1,
    )


def normalize(rows_in, norm_gain):
    widened = rows_in.astype(jnp.float32)
    inverse = lax.rsqrt(jnp.mean(widened * widened, axis=-1, keepdims=True) + 1e-06)
    return (widened * inverse * norm_gain.astype(jnp.float32)).astype(jnp.bfloat16)


def attend_kernel(q_ref, ko_ref, vo_ref, ka_ref, va_ref, kb_ref, vb_ref, bias_ref, out_ref):
    inv_root = 1.0 / math.sqrt(HD)
    q = q_ref[...]
    contract = (((1,), (1,)), ((), ()))
    own = lax.dot_general(q, ko_ref[...], contract, preferred_element_type=jnp.float32) * inv_root
    halves = []
    for index, (k_ref, v_ref) in enumerate(((ka_ref, va_ref), (kb_ref, vb_ref))):
        shards, ctx_rows, width = k_ref.shape
        keys = k_ref[...].reshape(shards * ctx_rows, width)
        values = v_ref[...].reshape(shards * ctx_rows, width)
        far = lax.dot_general(q, keys, contract, preferred_element_type=jnp.float32) * inv_root
        halves.append((far + bias_ref[index], values))
    highest = jnp.max(own, axis=-1, keepdims=True)
    for far, ignored in halves:
        highest = jnp.maximum(highest, jnp.max(far, axis=-1, keepdims=True))
    own_w = jnp.exp(own - highest)
    totals = jnp.sum(own_w, axis=-1, keepdims=True)
    mixture = jnp.dot(own_w.astype(jnp.bfloat16), vo_ref[...], preferred_element_type=jnp.float32)
    for far, values in halves:
        far_w = jnp.exp(far - highest)
        totals = totals + jnp.sum(far_w, axis=-1, keepdims=True)
        mixture = mixture + jnp.dot(far_w.astype(jnp.bfloat16), values, preferred_element_type=jnp.float32)
    out_ref[...] = (mixture / totals).astype(out_ref.dtype)


def attend(q_rot, k_rot, value_rows, own_half, other_half, bias, key_block, value_block):
    passes, rows, width = q_rot.shape
    heads = width // HD
    shards, ignored, lanes = own_half.shape
    ctx_rows = bias.shape[2] // shards
    cache_spec_k = pl.BlockSpec((shards, ctx_rows, lanes), lambda p, h: (0, key_block, 0))
    cache_spec_v = pl.BlockSpec((shards, ctx_rows, lanes), lambda p, h: (0, value_block, 0))
    ctx = 2 * shards * ctx_rows
    return pl.pallas_call(
        attend_kernel,
        grid=(passes, heads),
        in_specs=[
            pl.BlockSpec((None, rows, HD), lambda p, h: (p, 0, h)),
            pl.BlockSpec((None, rows, HD), lambda p, h: (p, 0, 0)),
            pl.BlockSpec((None, rows, HD), lambda p, h: (p, 0, 0)),
            cache_spec_k,
            cache_spec_v,
            cache_spec_k,
            cache_spec_v,
            pl.BlockSpec(bias.shape, lambda p, h: (0, 0, 0)),
        ],
        out_specs=pl.BlockSpec((None, rows, HD), lambda p, h: (p, 0, h)),
        out_shape=jax.ShapeDtypeStruct((passes, rows, width), jnp.bfloat16),
        cost_estimate=pl.CostEstimate(
            flops=4 * passes * heads * rows * (ctx + rows) * HD,
            transcendentals=passes * heads * rows * (ctx + rows),
            bytes_accessed=2 * (2 * ctx * HD + 4 * passes * rows * width),
        ),
    )(q_rot, k_rot, value_rows, own_half, own_half, other_half, other_half, bias)


def local(
    embeds,
    given_embeds,
    accept,
    lengths,
    block_keep,
    norm_gain,
    w_query,
    b_query,
    w_key,
    b_key,
    w_value,
    b_value,
    cache_keys,
    cache_values,
):
    local_kv = w_key.shape[1] // HD
    block_rows = embeds.shape[0]
    ctx_rows = cache_keys.shape[0]
    q_cols = w_query.shape[1]
    w_rows = w_query.shape[0]

    tp_size = lax.axis_size("tp")
    me_tp = lax.axis_index("tp")
    mine = jnp.stack([embeds, given_embeds])
    pieces = [mine]
    for shift in range(1, tp_size):
        pairs = [(i, (i - shift) % tp_size) for i in range(tp_size)]
        pieces.append(lax.ppermute(mine, "tp", pairs))
    ordered = jnp.roll(jnp.stack(pieces), me_tp, axis=0)
    both = jnp.concatenate([ordered[i] for i in range(tp_size)], axis=-1)
    first_rows, given_rows = both[0], both[1]

    w_parts = [w_query[:, j * HD : (j + 1) * HD] for j in range(q_cols // HD)] + [w_key, w_value]
    w_len = len(w_parts) * w_rows
    key_block = -(-w_len // ctx_rows)
    value_block = key_block + 1
    used = (value_block + 1) * ctx_rows
    total_blocks = -(-used // w_rows)
    lead = jnp.zeros((key_block * ctx_rows - w_len, HD), w_query.dtype)
    tail = jnp.zeros((total_blocks * w_rows - used, HD), w_query.dtype)
    packed = jnp.concatenate(w_parts + [lead, cache_keys, cache_values, tail], axis=0)
    own_half = lax.all_gather(packed, "chip", axis=0, tiled=False)
    other_half = lax.ppermute(own_half, "core", [(0, 1), (1, 0)])
    chips = own_half.shape[0]
    me_core = lax.axis_index("core")

    revised = jnp.where(accept[:, None] == 1, given_rows, first_rows)
    normed = normalize(jnp.concatenate([first_rows, revised], axis=0), norm_gain)
    normed4 = normed.reshape(normed.shape[0], chips, 2, w_rows)
    proj = None
    for half, core in ((own_half, me_core), (other_half, 1 - me_core)):
        part = jnp.einsum(
            "rsi,sjic->rjc",
            lax.dynamic_index_in_dim(normed4, core, axis=2, keepdims=False),
            half.reshape(chips, total_blocks, w_rows, HD),
            preferred_element_type=jnp.float32,
        )
        proj = part if proj is None else proj + part
    queries = proj[:, : q_cols // HD, :].reshape(-1, q_cols) + b_query.astype(jnp.float32)
    key_proj = proj[:, q_cols // HD, :] + b_key.astype(jnp.float32)
    value_proj = proj[:, q_cols // HD + 1, :] + b_value.astype(jnp.float32)
    length = lengths[0]
    keep_row = block_keep[0]
    positions = length.astype(jnp.float32) + jnp.arange(block_rows, dtype=jnp.float32)
    q_rot = rotate(queries.reshape(2, block_rows, q_cols // HD, HD), positions).astype(jnp.bfloat16)
    k_rot = rotate(key_proj.reshape(2, block_rows, local_kv, HD), positions).astype(jnp.bfloat16)
    value_rows = value_proj.astype(jnp.bfloat16)

    blocks_all = keep_row.shape[0]
    cache_index = jnp.arange(blocks_all * ctx_rows, dtype=jnp.int32).reshape(chips, 2, ctx_rows)
    kept = jnp.broadcast_to(keep_row.reshape(chips, 2, 1), cache_index.shape) == 1
    visible = (cache_index < length) & kept
    bias3 = jnp.where(visible, 0.0, -jnp.inf).astype(jnp.float32)
    bias = jnp.stack(
        [
            lax.dynamic_index_in_dim(bias3, me_core, axis=1, keepdims=False).reshape(1, -1),
            lax.dynamic_index_in_dim(bias3, 1 - me_core, axis=1, keepdims=False).reshape(1, -1),
        ]
    )
    attended = attend(
        q_rot.reshape(2, block_rows, q_cols),
        k_rot.reshape(2, block_rows, local_kv * HD),
        value_rows.reshape(2, block_rows, local_kv * HD),
        own_half,
        other_half,
        bias,
        key_block,
        value_block,
    )
    return (attended[0], attended[1])


def solution(mesh):
    blk_size, tp_size = mesh.devices.shape
    fine = Mesh(mesh.devices.reshape(blk_size // 2, 2, tp_size), ("chip", "core", "tp"))
    rows = ("chip", "core")
    return jax.shard_map(
        local,
        mesh=fine,
        in_specs=(
            P(rows, "tp"),
            P(rows, "tp"),
            P(rows),
            P(rows),
            P(rows, None),
            P(),
            P(rows, "tp"),
            P("tp"),
            P(rows, "tp"),
            P("tp"),
            P(rows, "tp"),
            P("tp"),
            P(rows, "tp"),
            P(rows, "tp"),
        ),
        out_specs=(P(rows, "tp"), P(rows, "tp")),
        check_vma=False,
    )
```

```python
import math

import jax
import jax.numpy as jnp
from jax import lax
from jax.experimental import pallas as pl
from jax.experimental.pallas import tpu as pltpu
from jax.sharding import Mesh
from jax.sharding import PartitionSpec as P

KVH = 8
HD = 128
HQ = 40
CB = 64


def rotate(vectors, positions):
    halfway = HD // 2
    frequency = 1000000.0 ** (-(jnp.arange(halfway, dtype=jnp.float32) * (2.0 / HD)))
    angles = positions[..., None] * frequency
    cosine = jnp.cos(angles)[..., None, :]
    sine_part = jnp.sin(angles)[..., None, :]
    front_part = vectors[..., :halfway]
    back_part = vectors[..., halfway:]
    return jnp.concatenate(
        [front_part * cosine - back_part * sine_part, back_part * cosine + front_part * sine_part],
        axis=-1,
    )


def normalize(rows_in, norm_gain):
    widened = rows_in.astype(jnp.float32)
    inverse = lax.rsqrt(jnp.mean(widened * widened, axis=-1, keepdims=True) + 1e-06)
    return (widened * inverse * norm_gain.astype(jnp.float32)).astype(jnp.bfloat16)


def attend_kernel(q_ref, ko_ref, vo_ref, kc_ref, vc_ref, bias_ref, out_ref):
    inv_root = 1.0 / math.sqrt(HD)
    q = q_ref[...]
    contract = (((1,), (1,)), ((), ()))
    own = lax.dot_general(q, ko_ref[...], contract, preferred_element_type=jnp.float32) * inv_root
    far = lax.dot_general(q, kc_ref[...], contract, preferred_element_type=jnp.float32) * inv_root
    far = far + bias_ref[...]
    highest = jnp.maximum(jnp.max(own, axis=-1, keepdims=True), jnp.max(far, axis=-1, keepdims=True))
    own_w = jnp.exp(own - highest)
    far_w = jnp.exp(far - highest)
    totals = jnp.sum(own_w, axis=-1, keepdims=True) + jnp.sum(far_w, axis=-1, keepdims=True)
    mixture = jnp.dot(own_w.astype(jnp.bfloat16), vo_ref[...], preferred_element_type=jnp.float32)
    mixture = mixture + jnp.dot(far_w.astype(jnp.bfloat16), vc_ref[...], preferred_element_type=jnp.float32)
    out_ref[...] = (mixture / totals).astype(out_ref.dtype)


def attend(q_rot, k_rot, value_rows, cache_k, cache_v, bias):
    passes, rows, width = q_rot.shape
    heads = width // HD
    ctx = cache_k.shape[0]
    return pl.pallas_call(
        attend_kernel,
        grid=(passes, heads),
        in_specs=[
            pl.BlockSpec((None, rows, HD), lambda p, h: (p, 0, h)),
            pl.BlockSpec((None, rows, HD), lambda p, h: (p, 0, 0)),
            pl.BlockSpec((None, rows, HD), lambda p, h: (p, 0, 0)),
            pl.BlockSpec((ctx, HD), lambda p, h: (0, 0)),
            pl.BlockSpec((ctx, HD), lambda p, h: (0, 0)),
            pl.BlockSpec((1, ctx), lambda p, h: (0, 0)),
        ],
        out_specs=pl.BlockSpec((None, rows, HD), lambda p, h: (p, 0, h)),
        out_shape=jax.ShapeDtypeStruct((passes, rows, width), jnp.bfloat16),
        cost_estimate=pl.CostEstimate(
            flops=4 * passes * heads * rows * (ctx + rows) * HD,
            transcendentals=passes * heads * rows * (ctx + rows),
            bytes_accessed=2 * (2 * ctx * HD + 4 * passes * rows * width),
        ),
    )(q_rot, k_rot, value_rows, cache_k, cache_v, bias)


def shifted(x, axis, size, shift):
    pairs = [(j, (j - shift) % size) for j in range(size)]
    return lax.ppermute(x, axis, pairs)


def local(
    embeds,
    given_embeds,
    accept,
    lengths,
    block_keep,
    norm_gain,
    w_query,
    b_query,
    w_key,
    b_key,
    w_value,
    b_value,
    cache_keys,
    cache_values,
):
    local_kv = w_key.shape[1] // HD
    block_rows = embeds.shape[0]
    ctx_rows = cache_keys.shape[0]
    q_cols = w_query.shape[1]
    w_rows = w_query.shape[0]

    tp_size = lax.axis_size("tp")
    me_tp = lax.axis_index("tp")
    mine = jnp.stack([embeds, given_embeds])
    pieces = [mine] + [shifted(mine, "tp", tp_size, k) for k in range(1, tp_size)]
    ordered = jnp.roll(jnp.stack(pieces), me_tp, axis=0)
    both = jnp.concatenate([ordered[i] for i in range(tp_size)], axis=-1)
    first_rows, given_rows = both[0], both[1]

    w_parts = [w_query[:, j * HD : (j + 1) * HD] for j in range(q_cols // HD)] + [w_key, w_value]
    w_len = len(w_parts) * w_rows
    key_start = -(-w_len // ctx_rows) * ctx_rows
    value_start = key_start + ctx_rows
    used = value_start + ctx_rows
    total_blocks = -(-used // w_rows)
    lead = jnp.zeros((key_start - w_len, HD), w_query.dtype)
    tail = jnp.zeros((total_blocks * w_rows - used, HD), w_query.dtype)
    packed = jnp.concatenate(w_parts + [lead, cache_keys, cache_values, tail], axis=0)

    n_ylo = lax.axis_size("ylo")
    n_z = lax.axis_size("z")
    me_ylo = lax.axis_index("ylo")
    me_z = lax.axis_index("z")
    me_core = lax.axis_index("core")

    line = jnp.stack([packed] + [shifted(packed, "ylo", n_ylo, k) for k in range(1, n_ylo)])
    arrived = [(0, line)]
    forward = line
    backward = line
    for step in range(1, n_z // 2 + 1):
        forward = shifted(forward, "z", n_z, -1)
        arrived.append((-step, forward))
        if step < n_z - n_z // 2:
            backward = shifted(backward, "z", n_z, 1)
            arrived.append((step, backward))
    held = [(offset, 0, piece) for offset, piece in arrived]
    held += [(offset, 1, shifted(piece, "core", 2, 1)) for offset, piece in arrived]

    revised = jnp.where(accept[:, None] == 1, given_rows, first_rows)
    normed = normalize(jnp.concatenate([first_rows, revised], axis=0), norm_gain)
    normed5 = normed.reshape(normed.shape[0], n_ylo, n_z, 2, w_rows)
    normed5 = jnp.roll(normed5, -me_ylo, axis=1)
    normed5 = jnp.roll(normed5, -me_z, axis=2)
    normed5 = jnp.roll(normed5, -me_core, axis=3)
    proj = None
    for offset, core, piece in held:
        part = jnp.einsum(
            "rki,kjid->rjd",
            normed5[:, :, offset % n_z, core, :],
            piece.reshape(n_ylo, total_blocks, w_rows, HD),
            preferred_element_type=jnp.float32,
        )
        proj = part if proj is None else proj + part
    queries = proj[:, : q_cols // HD, :].reshape(-1, q_cols) + b_query.astype(jnp.float32)
    key_proj = proj[:, q_cols // HD, :] + b_key.astype(jnp.float32)
    value_proj = proj[:, q_cols // HD + 1, :] + b_value.astype(jnp.float32)
    length = lengths[0]
    keep_row = block_keep[0]
    positions = length.astype(jnp.float32) + jnp.arange(block_rows, dtype=jnp.float32)
    q_rot = rotate(queries.reshape(2, block_rows, q_cols // HD, HD), positions).astype(jnp.bfloat16)
    k_rot = rotate(key_proj.reshape(2, block_rows, local_kv, HD), positions).astype(jnp.bfloat16)
    value_rows = value_proj.astype(jnp.bfloat16)

    blocks_all = keep_row.shape[0]
    cache_index = jnp.arange(blocks_all * ctx_rows, dtype=jnp.int32).reshape(n_ylo, n_z, 2, ctx_rows)
    kept = jnp.broadcast_to(keep_row.reshape(n_ylo, n_z, 2, 1), cache_index.shape) == 1
    visible = (cache_index < length) & kept
    bias4 = jnp.where(visible, 0.0, -jnp.inf).astype(jnp.float32)
    bias4 = jnp.roll(bias4, -me_ylo, axis=0)
    bias4 = jnp.roll(bias4, -me_z, axis=1)
    bias4 = jnp.roll(bias4, -me_core, axis=2)
    bias = jnp.concatenate([bias4[:, offset % n_z, core, :].reshape(1, -1) for offset, core, ignored in held], axis=1)
    cache_k = jnp.concatenate(
        [piece[:, key_start:value_start, :].reshape(-1, HD) for ignored, ignored2, piece in held], axis=0
    )
    cache_v = jnp.concatenate(
        [piece[:, value_start:used, :].reshape(-1, HD) for ignored, ignored2, piece in held], axis=0
    )
    attended = attend(
        q_rot.reshape(2, block_rows, q_cols),
        k_rot.reshape(2, block_rows, local_kv * HD),
        value_rows.reshape(2, block_rows, local_kv * HD),
        cache_k,
        cache_v,
        bias,
    )
    return (attended[0], attended[1])


def solution(mesh):
    blk_size, tp_size = mesh.devices.shape
    fine = Mesh(mesh.devices.reshape(4, blk_size // 8, 2, tp_size), ("ylo", "z", "core", "tp"))
    rows = ("ylo", "z", "core")
    return jax.shard_map(
        local,
        mesh=fine,
        in_specs=(
            P(rows, "tp"),
            P(rows, "tp"),
            P(rows),
            P(rows),
            P(rows, None),
            P(),
            P(rows, "tp"),
            P("tp"),
            P(rows, "tp"),
            P("tp"),
            P(rows, "tp"),
            P("tp"),
            P(rows, "tp"),
            P(rows, "tp"),
        ),
        out_specs=(P(rows, "tp"), P(rows, "tp")),
        check_vma=False,
    )
```

```python
import math

import jax
import jax.numpy as jnp
from jax import lax
from jax.experimental import pallas as pl
from jax.experimental.pallas import tpu as pltpu
from jax.sharding import Mesh
from jax.sharding import PartitionSpec as P

KVH = 8
HD = 128
HQ = 40
CB = 64


def rotate(vectors, positions):
    halfway = HD // 2
    frequency = 1000000.0 ** (-(jnp.arange(halfway, dtype=jnp.float32) * (2.0 / HD)))
    angles = positions[..., None] * frequency
    cosine = jnp.cos(angles)[..., None, :]
    sine_part = jnp.sin(angles)[..., None, :]
    front_part = vectors[..., :halfway]
    back_part = vectors[..., halfway:]
    return jnp.concatenate(
        [front_part * cosine - back_part * sine_part, back_part * cosine + front_part * sine_part],
        axis=-1,
    )


def normalize(rows_in, norm_gain):
    widened = rows_in.astype(jnp.float32)
    inverse = lax.rsqrt(jnp.mean(widened * widened, axis=-1, keepdims=True) + 1e-06)
    return (widened * inverse * norm_gain.astype(jnp.float32)).astype(jnp.bfloat16)


def attend_kernel(q_ref, ko_ref, vo_ref, kc_ref, vc_ref, bias_ref, out_ref):
    inv_root = 1.0 / math.sqrt(HD)
    q = q_ref[...]
    contract = (((1,), (1,)), ((), ()))
    own = lax.dot_general(q, ko_ref[...], contract, preferred_element_type=jnp.float32) * inv_root
    far = lax.dot_general(q, kc_ref[...], contract, preferred_element_type=jnp.float32) * inv_root
    far = far + bias_ref[...]
    highest = jnp.maximum(jnp.max(own, axis=-1, keepdims=True), jnp.max(far, axis=-1, keepdims=True))
    own_w = jnp.exp(own - highest)
    far_w = jnp.exp(far - highest)
    totals = jnp.sum(own_w, axis=-1, keepdims=True) + jnp.sum(far_w, axis=-1, keepdims=True)
    mixture = jnp.dot(own_w.astype(jnp.bfloat16), vo_ref[...], preferred_element_type=jnp.float32)
    mixture = mixture + jnp.dot(far_w.astype(jnp.bfloat16), vc_ref[...], preferred_element_type=jnp.float32)
    out_ref[...] = (mixture / totals).astype(out_ref.dtype)


def attend(q_rot, k_rot, value_rows, cache_k, cache_v, bias):
    passes, rows, width = q_rot.shape
    heads = width // HD
    ctx = cache_k.shape[0]
    return pl.pallas_call(
        attend_kernel,
        grid=(passes, heads),
        in_specs=[
            pl.BlockSpec((None, rows, HD), lambda p, h: (p, 0, h)),
            pl.BlockSpec((None, rows, HD), lambda p, h: (p, 0, 0)),
            pl.BlockSpec((None, rows, HD), lambda p, h: (p, 0, 0)),
            pl.BlockSpec((ctx, HD), lambda p, h: (0, 0)),
            pl.BlockSpec((ctx, HD), lambda p, h: (0, 0)),
            pl.BlockSpec((1, ctx), lambda p, h: (0, 0)),
        ],
        out_specs=pl.BlockSpec((None, rows, HD), lambda p, h: (p, 0, h)),
        out_shape=jax.ShapeDtypeStruct((passes, rows, width), jnp.bfloat16),
        cost_estimate=pl.CostEstimate(
            flops=4 * passes * heads * rows * (ctx + rows) * HD,
            transcendentals=passes * heads * rows * (ctx + rows),
            bytes_accessed=2 * (2 * ctx * HD + 4 * passes * rows * width),
        ),
    )(q_rot, k_rot, value_rows, cache_k, cache_v, bias)


def shifted(x, axis, size, shift):
    pairs = [(j, (j - shift) % size) for j in range(size)]
    return lax.ppermute(x, axis, pairs)


def local(
    embeds,
    given_embeds,
    accept,
    lengths,
    block_keep,
    norm_gain,
    w_query,
    b_query,
    w_key,
    b_key,
    w_value,
    b_value,
    cache_keys,
    cache_values,
):
    local_kv = w_key.shape[1] // HD
    block_rows = embeds.shape[0]
    ctx_rows = cache_keys.shape[0]
    q_cols = w_query.shape[1]
    w_rows = w_query.shape[0]

    w_parts = [w_query[:, j * HD : (j + 1) * HD] for j in range(q_cols // HD)] + [w_key, w_value]
    w_len = len(w_parts) * w_rows
    key_start = -(-w_len // ctx_rows) * ctx_rows
    value_start = key_start + ctx_rows
    used = value_start + ctx_rows
    total_blocks = -(-used // w_rows)
    lead = jnp.zeros((key_start - w_len, HD), w_query.dtype)
    tail = jnp.zeros((total_blocks * w_rows - used, HD), w_query.dtype)
    packed = jnp.concatenate(w_parts + [lead, cache_keys, cache_values, tail], axis=0)

    n_ylo = lax.axis_size("ylo")
    n_z = lax.axis_size("z")
    me_ylo = lax.axis_index("ylo")
    me_z = lax.axis_index("z")
    me_core = lax.axis_index("core")

    line = jnp.stack([packed] + [shifted(packed, "ylo", n_ylo, k) for k in range(1, n_ylo)])
    arrived = [(0, line)]
    forward = line
    backward = line
    far = n_z // 2
    split = n_ylo // 2
    for step in range(1, far):
        forward = shifted(forward, "z", n_z, -1)
        backward = shifted(backward, "z", n_z, 1)
        arrived += [(-step, forward), (step, backward)]
    far_front = shifted(forward[:split], "z", n_z, -1)
    far_back = shifted(backward[split:], "z", n_z, 1)
    arrived.append((far, jnp.concatenate([far_front, far_back], axis=0)))
    held = [(offset, 0, piece) for offset, piece in arrived]
    held += [(offset, 1, shifted(piece, "core", 2, 1)) for offset, piece in arrived]

    mine = jnp.stack([embeds, given_embeds])
    mine, ignored = lax.optimization_barrier((mine, line))
    both = lax.all_gather(mine, "tp", axis=2, tiled=True)
    first_rows, given_rows = both[0], both[1]

    revised = jnp.where(accept[:, None] == 1, given_rows, first_rows)
    normed = normalize(jnp.concatenate([first_rows, revised], axis=0), norm_gain)
    normed5 = normed.reshape(normed.shape[0], n_ylo, n_z, 2, w_rows)
    normed5 = jnp.roll(normed5, -me_ylo, axis=1)
    normed5 = jnp.roll(normed5, -me_z, axis=2)
    normed5 = jnp.roll(normed5, -me_core, axis=3)
    proj = None
    for offset, core, piece in held:
        part = jnp.einsum(
            "rki,kjid->rjd",
            normed5[:, :, offset % n_z, core, :],
            piece.reshape(n_ylo, total_blocks, w_rows, HD),
            preferred_element_type=jnp.float32,
        )
        proj = part if proj is None else proj + part
    queries = proj[:, : q_cols // HD, :].reshape(-1, q_cols) + b_query.astype(jnp.float32)
    key_proj = proj[:, q_cols // HD, :] + b_key.astype(jnp.float32)
    value_proj = proj[:, q_cols // HD + 1, :] + b_value.astype(jnp.float32)
    length = lengths[0]
    keep_row = block_keep[0]
    positions = length.astype(jnp.float32) + jnp.arange(block_rows, dtype=jnp.float32)
    q_rot = rotate(queries.reshape(2, block_rows, q_cols // HD, HD), positions).astype(jnp.bfloat16)
    k_rot = rotate(key_proj.reshape(2, block_rows, local_kv, HD), positions).astype(jnp.bfloat16)
    value_rows = value_proj.astype(jnp.bfloat16)

    blocks_all = keep_row.shape[0]
    cache_index = jnp.arange(blocks_all * ctx_rows, dtype=jnp.int32).reshape(n_ylo, n_z, 2, ctx_rows)
    kept = jnp.broadcast_to(keep_row.reshape(n_ylo, n_z, 2, 1), cache_index.shape) == 1
    visible = (cache_index < length) & kept
    bias4 = jnp.where(visible, 0.0, -jnp.inf).astype(jnp.float32)
    bias4 = jnp.roll(bias4, -me_ylo, axis=0)
    bias4 = jnp.roll(bias4, -me_z, axis=1)
    bias4 = jnp.roll(bias4, -me_core, axis=2)
    bias = jnp.concatenate([bias4[:, offset % n_z, core, :].reshape(1, -1) for offset, core, ignored in held], axis=1)
    cache_k = jnp.concatenate(
        [piece[:, key_start:value_start, :].reshape(-1, HD) for ignored, ignored2, piece in held], axis=0
    )
    cache_v = jnp.concatenate(
        [piece[:, value_start:used, :].reshape(-1, HD) for ignored, ignored2, piece in held], axis=0
    )
    attended = attend(
        q_rot.reshape(2, block_rows, q_cols),
        k_rot.reshape(2, block_rows, local_kv * HD),
        value_rows.reshape(2, block_rows, local_kv * HD),
        cache_k,
        cache_v,
        bias,
    )
    return (attended[0], attended[1])


def solution(mesh):
    blk_size, tp_size = mesh.devices.shape
    fine = Mesh(mesh.devices.reshape(4, blk_size // 8, 2, tp_size), ("ylo", "z", "core", "tp"))
    rows = ("ylo", "z", "core")
    return jax.shard_map(
        local,
        mesh=fine,
        in_specs=(
            P(rows, "tp"),
            P(rows, "tp"),
            P(rows),
            P(rows),
            P(rows, None),
            P(),
            P(rows, "tp"),
            P("tp"),
            P(rows, "tp"),
            P("tp"),
            P(rows, "tp"),
            P("tp"),
            P(rows, "tp"),
            P(rows, "tp"),
        ),
        out_specs=(P(rows, "tp"), P(rows, "tp")),
        check_vma=False,
    )
```

```python
import math

import jax
import jax.numpy as jnp
from jax import lax
from jax.experimental import pallas as pl
from jax.experimental.pallas import tpu as pltpu
from jax.sharding import Mesh
from jax.sharding import PartitionSpec as P

KVH = 8
HD = 128
HQ = 40
CB = 64


def rotate(vectors, positions):
    halfway = HD // 2
    frequency = 1000000.0 ** (-(jnp.arange(halfway, dtype=jnp.float32) * (2.0 / HD)))
    angles = positions[..., None] * frequency
    cosine = jnp.cos(angles)[..., None, :]
    sine_part = jnp.sin(angles)[..., None, :]
    front_part = vectors[..., :halfway]
    back_part = vectors[..., halfway:]
    return jnp.concatenate(
        [front_part * cosine - back_part * sine_part, back_part * cosine + front_part * sine_part],
        axis=-1,
    )


def normalize(rows_in, norm_gain):
    widened = rows_in.astype(jnp.float32)
    inverse = lax.rsqrt(jnp.mean(widened * widened, axis=-1, keepdims=True) + 1e-06)
    return (widened * inverse * norm_gain.astype(jnp.float32)).astype(jnp.bfloat16)


def attend_kernel(q_ref, ko_ref, vo_ref, kc_ref, vc_ref, bias_ref, out_ref):
    inv_root = 1.0 / math.sqrt(HD)
    q = q_ref[...]
    contract = (((1,), (1,)), ((), ()))
    own = lax.dot_general(q, ko_ref[...], contract, preferred_element_type=jnp.float32) * inv_root
    far = lax.dot_general(q, kc_ref[...], contract, preferred_element_type=jnp.float32) * inv_root
    far = far + bias_ref[...]
    highest = jnp.maximum(jnp.max(own, axis=-1, keepdims=True), jnp.max(far, axis=-1, keepdims=True))
    own_w = jnp.exp(own - highest)
    far_w = jnp.exp(far - highest)
    totals = jnp.sum(own_w, axis=-1, keepdims=True) + jnp.sum(far_w, axis=-1, keepdims=True)
    mixture = jnp.dot(own_w.astype(jnp.bfloat16), vo_ref[...], preferred_element_type=jnp.float32)
    mixture = mixture + jnp.dot(far_w.astype(jnp.bfloat16), vc_ref[...], preferred_element_type=jnp.float32)
    out_ref[...] = (mixture / totals).astype(out_ref.dtype)


def attend(q_rot, k_rot, value_rows, cache_k, cache_v, bias):
    passes, rows, width = q_rot.shape
    heads = width // HD
    ctx = cache_k.shape[0]
    return pl.pallas_call(
        attend_kernel,
        grid=(passes, heads),
        in_specs=[
            pl.BlockSpec((None, rows, HD), lambda p, h: (p, 0, h)),
            pl.BlockSpec((None, rows, HD), lambda p, h: (p, 0, 0)),
            pl.BlockSpec((None, rows, HD), lambda p, h: (p, 0, 0)),
            pl.BlockSpec((ctx, HD), lambda p, h: (0, 0)),
            pl.BlockSpec((ctx, HD), lambda p, h: (0, 0)),
            pl.BlockSpec((1, ctx), lambda p, h: (0, 0)),
        ],
        out_specs=pl.BlockSpec((None, rows, HD), lambda p, h: (p, 0, h)),
        out_shape=jax.ShapeDtypeStruct((passes, rows, width), jnp.bfloat16),
        cost_estimate=pl.CostEstimate(
            flops=4 * passes * heads * rows * (ctx + rows) * HD,
            transcendentals=passes * heads * rows * (ctx + rows),
            bytes_accessed=2 * (2 * ctx * HD + 4 * passes * rows * width),
        ),
    )(q_rot, k_rot, value_rows, cache_k, cache_v, bias)


def shifted(x, axis, size, shift):
    pairs = [(j, (j - shift) % size) for j in range(size)]
    return lax.ppermute(x, axis, pairs)


def local(
    embeds,
    given_embeds,
    accept,
    lengths,
    block_keep,
    norm_gain,
    w_query,
    b_query,
    w_key,
    b_key,
    w_value,
    b_value,
    cache_keys,
    cache_values,
):
    local_kv = w_key.shape[1] // HD
    block_rows = embeds.shape[0]
    ctx_rows = cache_keys.shape[0]
    q_cols = w_query.shape[1]
    w_rows = w_query.shape[0]

    w_parts = [w_query[:, j * HD : (j + 1) * HD] for j in range(q_cols // HD)] + [w_key, w_value]
    w_len = len(w_parts) * w_rows
    key_start = -(-w_len // ctx_rows) * ctx_rows
    value_start = key_start + ctx_rows
    used = value_start + ctx_rows
    total_blocks = -(-used // w_rows)
    lead = jnp.zeros((key_start - w_len, HD), w_query.dtype)
    tail = jnp.zeros((total_blocks * w_rows - used, HD), w_query.dtype)
    packed = jnp.concatenate(w_parts + [lead, cache_keys, cache_values, tail], axis=0)

    n_ylo = lax.axis_size("ylo")
    n_z = lax.axis_size("z")
    me_ylo = lax.axis_index("ylo")
    me_z = lax.axis_index("z")
    me_core = lax.axis_index("core")

    mine = jnp.stack([embeds, given_embeds])
    both = lax.all_gather(mine, "tp", axis=2, tiled=True)
    first_rows, given_rows = both[0], both[1]

    revised = jnp.where(accept[:, None] == 1, given_rows, first_rows)
    normed = normalize(jnp.concatenate([first_rows, revised], axis=0), norm_gain)
    normed5 = normed.reshape(normed.shape[0], n_ylo, n_z, 2, w_rows)
    normed5 = jnp.roll(normed5, -me_ylo, axis=1)
    normed5 = jnp.roll(normed5, -me_z, axis=2)
    normed5 = jnp.roll(normed5, -me_core, axis=3)
    line = jnp.stack([packed] + [shifted(packed, "ylo", n_ylo, k) for k in range(1, n_ylo)])
    arrived = [(0, line)]
    forward = line
    backward = line
    far = n_z // 2
    split = n_ylo // 2
    for step in range(1, far):
        forward = shifted(forward, "z", n_z, -1)
        backward = shifted(backward, "z", n_z, 1)
        arrived += [(-step, forward), (step, backward)]
    normed5, forward, backward = lax.optimization_barrier((normed5, forward, backward))
    far_front = shifted(forward[:split], "z", n_z, -1)
    far_back = shifted(backward[split:], "z", n_z, 1)
    arrived.append((far, jnp.concatenate([far_front, far_back], axis=0)))
    held = [(offset, 0, piece) for offset, piece in arrived]
    held += [(offset, 1, shifted(piece, "core", 2, 1)) for offset, piece in arrived]

    proj = None
    for offset, core, piece in held:
        part = jnp.einsum(
            "rki,kjid->rjd",
            normed5[:, :, offset % n_z, core, :],
            piece.reshape(n_ylo, total_blocks, w_rows, HD),
            preferred_element_type=jnp.float32,
        )
        proj = part if proj is None else proj + part
    queries = proj[:, : q_cols // HD, :].reshape(-1, q_cols) + b_query.astype(jnp.float32)
    key_proj = proj[:, q_cols // HD, :] + b_key.astype(jnp.float32)
    value_proj = proj[:, q_cols // HD + 1, :] + b_value.astype(jnp.float32)
    length = lengths[0]
    keep_row = block_keep[0]
    positions = length.astype(jnp.float32) + jnp.arange(block_rows, dtype=jnp.float32)
    q_rot = rotate(queries.reshape(2, block_rows, q_cols // HD, HD), positions).astype(jnp.bfloat16)
    k_rot = rotate(key_proj.reshape(2, block_rows, local_kv, HD), positions).astype(jnp.bfloat16)
    value_rows = value_proj.astype(jnp.bfloat16)

    blocks_all = keep_row.shape[0]
    cache_index = jnp.arange(blocks_all * ctx_rows, dtype=jnp.int32).reshape(n_ylo, n_z, 2, ctx_rows)
    kept = jnp.broadcast_to(keep_row.reshape(n_ylo, n_z, 2, 1), cache_index.shape) == 1
    visible = (cache_index < length) & kept
    bias4 = jnp.where(visible, 0.0, -jnp.inf).astype(jnp.float32)
    bias4 = jnp.roll(bias4, -me_ylo, axis=0)
    bias4 = jnp.roll(bias4, -me_z, axis=1)
    bias4 = jnp.roll(bias4, -me_core, axis=2)
    bias = jnp.concatenate([bias4[:, offset % n_z, core, :].reshape(1, -1) for offset, core, ignored in held], axis=1)
    cache_k = jnp.concatenate(
        [piece[:, key_start:value_start, :].reshape(-1, HD) for ignored, ignored2, piece in held], axis=0
    )
    cache_v = jnp.concatenate(
        [piece[:, value_start:used, :].reshape(-1, HD) for ignored, ignored2, piece in held], axis=0
    )
    attended = attend(
        q_rot.reshape(2, block_rows, q_cols),
        k_rot.reshape(2, block_rows, local_kv * HD),
        value_rows.reshape(2, block_rows, local_kv * HD),
        cache_k,
        cache_v,
        bias,
    )
    return (attended[0], attended[1])


def solution(mesh):
    blk_size, tp_size = mesh.devices.shape
    fine = Mesh(mesh.devices.reshape(4, blk_size // 8, 2, tp_size), ("ylo", "z", "core", "tp"))
    rows = ("ylo", "z", "core")
    return jax.shard_map(
        local,
        mesh=fine,
        in_specs=(
            P(rows, "tp"),
            P(rows, "tp"),
            P(rows),
            P(rows),
            P(rows, None),
            P(),
            P(rows, "tp"),
            P("tp"),
            P(rows, "tp"),
            P("tp"),
            P(rows, "tp"),
            P("tp"),
            P(rows, "tp"),
            P(rows, "tp"),
        ),
        out_specs=(P(rows, "tp"), P(rows, "tp")),
        check_vma=False,
    )
```

```python
import math

import jax
import jax.numpy as jnp
from jax import lax
from jax.experimental import pallas as pl
from jax.experimental.pallas import tpu as pltpu
from jax.sharding import Mesh
from jax.sharding import PartitionSpec as P

KVH = 8
HD = 128
HQ = 40
CB = 64


def rotate(vectors, positions):
    halfway = HD // 2
    frequency = 1000000.0 ** (-(jnp.arange(halfway, dtype=jnp.float32) * (2.0 / HD)))
    angles = positions[..., None] * frequency
    cosine = jnp.cos(angles)[..., None, :]
    sine_part = jnp.sin(angles)[..., None, :]
    front_part = vectors[..., :halfway]
    back_part = vectors[..., halfway:]
    return jnp.concatenate(
        [front_part * cosine - back_part * sine_part, back_part * cosine + front_part * sine_part],
        axis=-1,
    )


def normalize(rows_in, norm_gain):
    widened = rows_in.astype(jnp.float32)
    inverse = lax.rsqrt(jnp.mean(widened * widened, axis=-1, keepdims=True) + 1e-06)
    return (widened * inverse * norm_gain.astype(jnp.float32)).astype(jnp.bfloat16)


def attend_kernel(q_ref, ko_ref, vo_ref, kc_ref, vc_ref, bias_ref, out_ref):
    inv_root = 1.0 / math.sqrt(HD)
    q = q_ref[...]
    contract = (((1,), (1,)), ((), ()))
    own = lax.dot_general(q, ko_ref[...], contract, preferred_element_type=jnp.float32) * inv_root
    far = lax.dot_general(q, kc_ref[...], contract, preferred_element_type=jnp.float32) * inv_root
    far = far + bias_ref[...]
    highest = jnp.maximum(jnp.max(own, axis=-1, keepdims=True), jnp.max(far, axis=-1, keepdims=True))
    own_w = jnp.exp(own - highest)
    far_w = jnp.exp(far - highest)
    totals = jnp.sum(own_w, axis=-1, keepdims=True) + jnp.sum(far_w, axis=-1, keepdims=True)
    mixture = jnp.dot(own_w.astype(jnp.bfloat16), vo_ref[...], preferred_element_type=jnp.float32)
    mixture = mixture + jnp.dot(far_w.astype(jnp.bfloat16), vc_ref[...], preferred_element_type=jnp.float32)
    out_ref[...] = (mixture / totals).astype(out_ref.dtype)


def attend(q_rot, k_rot, value_rows, cache_k, cache_v, bias):
    passes, rows, width = q_rot.shape
    heads = width // HD
    ctx = cache_k.shape[0]
    return pl.pallas_call(
        attend_kernel,
        grid=(passes, heads),
        in_specs=[
            pl.BlockSpec((None, rows, HD), lambda p, h: (p, 0, h)),
            pl.BlockSpec((None, rows, HD), lambda p, h: (p, 0, 0)),
            pl.BlockSpec((None, rows, HD), lambda p, h: (p, 0, 0)),
            pl.BlockSpec((ctx, HD), lambda p, h: (0, 0)),
            pl.BlockSpec((ctx, HD), lambda p, h: (0, 0)),
            pl.BlockSpec((1, ctx), lambda p, h: (0, 0)),
        ],
        out_specs=pl.BlockSpec((None, rows, HD), lambda p, h: (p, 0, h)),
        out_shape=jax.ShapeDtypeStruct((passes, rows, width), jnp.bfloat16),
        cost_estimate=pl.CostEstimate(
            flops=4 * passes * heads * rows * (ctx + rows) * HD,
            transcendentals=passes * heads * rows * (ctx + rows),
            bytes_accessed=2 * (2 * ctx * HD + 4 * passes * rows * width),
        ),
    )(q_rot, k_rot, value_rows, cache_k, cache_v, bias)


def shifted(x, axis, size, shift):
    pairs = [(j, (j - shift) % size) for j in range(size)]
    return lax.ppermute(x, axis, pairs)


def local(
    embeds,
    given_embeds,
    accept,
    lengths,
    block_keep,
    norm_gain,
    w_query,
    b_query,
    w_key,
    b_key,
    w_value,
    b_value,
    cache_keys,
    cache_values,
):
    local_kv = w_key.shape[1] // HD
    block_rows = embeds.shape[0]
    ctx_rows = cache_keys.shape[0]
    q_cols = w_query.shape[1]
    w_rows = w_query.shape[0]

    w_parts = [w_query[:, j * HD : (j + 1) * HD] for j in range(q_cols // HD)] + [w_key, w_value]
    w_len = len(w_parts) * w_rows
    key_start = -(-w_len // ctx_rows) * ctx_rows
    value_start = key_start + ctx_rows
    used = value_start + ctx_rows
    total_blocks = -(-used // w_rows)
    lead = jnp.zeros((key_start - w_len, HD), w_query.dtype)
    tail = jnp.zeros((total_blocks * w_rows - used, HD), w_query.dtype)
    packed = jnp.concatenate(w_parts + [lead, cache_keys, cache_values, tail], axis=0)

    n_ylo = lax.axis_size("ylo")
    n_z = lax.axis_size("z")
    me_ylo = lax.axis_index("ylo")
    me_z = lax.axis_index("z")
    me_core = lax.axis_index("core")

    mine = jnp.stack([embeds, given_embeds])
    both = lax.all_gather(mine, "tp", axis=2, tiled=True)
    first_rows, given_rows = both[0], both[1]

    revised = jnp.where(accept[:, None] == 1, given_rows, first_rows)
    normed = normalize(jnp.concatenate([first_rows, revised], axis=0), norm_gain)
    normed5 = normed.reshape(normed.shape[0], n_ylo, n_z, 2, w_rows)
    normed5 = jnp.roll(normed5, -me_ylo, axis=1)
    normed5 = jnp.roll(normed5, -me_z, axis=2)
    normed5 = jnp.roll(normed5, -me_core, axis=3)
    line = jnp.stack([packed] + [shifted(packed, "ylo", n_ylo, k) for k in range(1, n_ylo)])
    arrived = [(0, line)]
    forward = line
    backward = line
    far = n_z // 2
    split = n_ylo // 2
    for step in range(1, far):
        forward = shifted(forward, "z", n_z, -1)
        backward = shifted(backward, "z", n_z, 1)
        arrived += [(-step, forward), (step, backward)]
    far_front = shifted(forward[:split], "z", n_z, -1)
    far_back = shifted(backward[split:], "z", n_z, 1)
    normed5, far_front, far_back = lax.optimization_barrier((normed5, far_front, far_back))
    arrived.append((far, jnp.concatenate([far_front, far_back], axis=0)))
    held = [(offset, 0, piece) for offset, piece in arrived]
    held += [(offset, 1, shifted(piece, "core", 2, 1)) for offset, piece in arrived]

    proj = None
    for offset, core, piece in held:
        part = jnp.einsum(
            "rki,kjid->rjd",
            normed5[:, :, offset % n_z, core, :],
            piece.reshape(n_ylo, total_blocks, w_rows, HD),
            preferred_element_type=jnp.float32,
        )
        proj = part if proj is None else proj + part
    queries = proj[:, : q_cols // HD, :].reshape(-1, q_cols) + b_query.astype(jnp.float32)
    key_proj = proj[:, q_cols // HD, :] + b_key.astype(jnp.float32)
    value_proj = proj[:, q_cols // HD + 1, :] + b_value.astype(jnp.float32)
    length = lengths[0]
    keep_row = block_keep[0]
    positions = length.astype(jnp.float32) + jnp.arange(block_rows, dtype=jnp.float32)
    q_rot = rotate(queries.reshape(2, block_rows, q_cols // HD, HD), positions).astype(jnp.bfloat16)
    k_rot = rotate(key_proj.reshape(2, block_rows, local_kv, HD), positions).astype(jnp.bfloat16)
    value_rows = value_proj.astype(jnp.bfloat16)

    blocks_all = keep_row.shape[0]
    cache_index = jnp.arange(blocks_all * ctx_rows, dtype=jnp.int32).reshape(n_ylo, n_z, 2, ctx_rows)
    kept = jnp.broadcast_to(keep_row.reshape(n_ylo, n_z, 2, 1), cache_index.shape) == 1
    visible = (cache_index < length) & kept
    bias4 = jnp.where(visible, 0.0, -jnp.inf).astype(jnp.float32)
    bias4 = jnp.roll(bias4, -me_ylo, axis=0)
    bias4 = jnp.roll(bias4, -me_z, axis=1)
    bias4 = jnp.roll(bias4, -me_core, axis=2)
    bias = jnp.concatenate([bias4[:, offset % n_z, core, :].reshape(1, -1) for offset, core, ignored in held], axis=1)
    cache_k = jnp.concatenate(
        [piece[:, key_start:value_start, :].reshape(-1, HD) for ignored, ignored2, piece in held], axis=0
    )
    cache_v = jnp.concatenate(
        [piece[:, value_start:used, :].reshape(-1, HD) for ignored, ignored2, piece in held], axis=0
    )
    attended = attend(
        q_rot.reshape(2, block_rows, q_cols),
        k_rot.reshape(2, block_rows, local_kv * HD),
        value_rows.reshape(2, block_rows, local_kv * HD),
        cache_k,
        cache_v,
        bias,
    )
    return (attended[0], attended[1])


def solution(mesh):
    blk_size, tp_size = mesh.devices.shape
    fine = Mesh(mesh.devices.reshape(4, blk_size // 8, 2, tp_size), ("ylo", "z", "core", "tp"))
    rows = ("ylo", "z", "core")
    return jax.shard_map(
        local,
        mesh=fine,
        in_specs=(
            P(rows, "tp"),
            P(rows, "tp"),
            P(rows),
            P(rows),
            P(rows, None),
            P(),
            P(rows, "tp"),
            P("tp"),
            P(rows, "tp"),
            P("tp"),
            P(rows, "tp"),
            P("tp"),
            P(rows, "tp"),
            P(rows, "tp"),
        ),
        out_specs=(P(rows, "tp"), P(rows, "tp")),
        check_vma=False,
    )
```

```python
import math

import jax
import jax.numpy as jnp
from jax import lax
from jax.experimental import pallas as pl
from jax.experimental.pallas import tpu as pltpu
from jax.sharding import Mesh
from jax.sharding import PartitionSpec as P

KVH = 8
HD = 128
HQ = 40
CB = 64


def rotate(vectors, positions):
    halfway = HD // 2
    frequency = 1000000.0 ** (-(jnp.arange(halfway, dtype=jnp.float32) * (2.0 / HD)))
    angles = positions[..., None] * frequency
    cosine = jnp.cos(angles)[..., None, :]
    sine_part = jnp.sin(angles)[..., None, :]
    front_part = vectors[..., :halfway]
    back_part = vectors[..., halfway:]
    return jnp.concatenate(
        [front_part * cosine - back_part * sine_part, back_part * cosine + front_part * sine_part],
        axis=-1,
    )


def normalize(rows_in, norm_gain):
    widened = rows_in.astype(jnp.float32)
    inverse = lax.rsqrt(jnp.mean(widened * widened, axis=-1, keepdims=True) + 1e-06)
    return (widened * inverse * norm_gain.astype(jnp.float32)).astype(jnp.bfloat16)


def attend_kernel(q_ref, ko_ref, vo_ref, kc_ref, vc_ref, bias_ref, out_ref):
    inv_root = 1.0 / math.sqrt(HD)
    q = q_ref[...]
    contract = (((1,), (1,)), ((), ()))
    own = lax.dot_general(q, ko_ref[...], contract, preferred_element_type=jnp.float32) * inv_root
    far = lax.dot_general(q, kc_ref[...], contract, preferred_element_type=jnp.float32) * inv_root
    far = far + bias_ref[...]
    highest = jnp.maximum(jnp.max(own, axis=-1, keepdims=True), jnp.max(far, axis=-1, keepdims=True))
    own_w = jnp.exp(own - highest)
    far_w = jnp.exp(far - highest)
    totals = jnp.sum(own_w, axis=-1, keepdims=True) + jnp.sum(far_w, axis=-1, keepdims=True)
    mixture = jnp.dot(own_w.astype(jnp.bfloat16), vo_ref[...], preferred_element_type=jnp.float32)
    mixture = mixture + jnp.dot(far_w.astype(jnp.bfloat16), vc_ref[...], preferred_element_type=jnp.float32)
    out_ref[...] = (mixture / totals).astype(out_ref.dtype)


def attend(q_rot, k_rot, value_rows, cache_k, cache_v, bias):
    passes, rows, width = q_rot.shape
    heads = width // HD
    ctx = cache_k.shape[0]
    return pl.pallas_call(
        attend_kernel,
        grid=(passes, heads),
        in_specs=[
            pl.BlockSpec((None, rows, HD), lambda p, h: (p, 0, h)),
            pl.BlockSpec((None, rows, HD), lambda p, h: (p, 0, 0)),
            pl.BlockSpec((None, rows, HD), lambda p, h: (p, 0, 0)),
            pl.BlockSpec((ctx, HD), lambda p, h: (0, 0)),
            pl.BlockSpec((ctx, HD), lambda p, h: (0, 0)),
            pl.BlockSpec((1, ctx), lambda p, h: (0, 0)),
        ],
        out_specs=pl.BlockSpec((None, rows, HD), lambda p, h: (p, 0, h)),
        out_shape=jax.ShapeDtypeStruct((passes, rows, width), jnp.bfloat16),
        cost_estimate=pl.CostEstimate(
            flops=4 * passes * heads * rows * (ctx + rows) * HD,
            transcendentals=passes * heads * rows * (ctx + rows),
            bytes_accessed=2 * (2 * ctx * HD + 4 * passes * rows * width),
        ),
    )(q_rot, k_rot, value_rows, cache_k, cache_v, bias)


def shifted(x, axis, size, shift):
    pairs = [(j, (j - shift) % size) for j in range(size)]
    return lax.ppermute(x, axis, pairs)


def local(
    embeds,
    given_embeds,
    accept,
    lengths,
    block_keep,
    norm_gain,
    w_query,
    b_query,
    w_key,
    b_key,
    w_value,
    b_value,
    cache_keys,
    cache_values,
):
    local_kv = w_key.shape[1] // HD
    block_rows = embeds.shape[0]
    ctx_rows = cache_keys.shape[0]
    q_cols = w_query.shape[1]
    w_rows = w_query.shape[0]

    w_parts = [w_query[:, j * HD : (j + 1) * HD] for j in range(q_cols // HD)] + [w_key, w_value]
    w_len = len(w_parts) * w_rows
    key_start = -(-w_len // ctx_rows) * ctx_rows
    value_start = key_start + ctx_rows
    used = value_start + ctx_rows
    total_blocks = -(-used // w_rows)
    lead = jnp.zeros((key_start - w_len, HD), w_query.dtype)
    tail = jnp.zeros((total_blocks * w_rows - used, HD), w_query.dtype)
    packed = jnp.concatenate(w_parts + [lead, cache_keys, cache_values, tail], axis=0)

    n_ylo = lax.axis_size("ylo")
    n_z = lax.axis_size("z")
    me_ylo = lax.axis_index("ylo")
    me_z = lax.axis_index("z")
    me_core = lax.axis_index("core")

    mine = jnp.stack([embeds, given_embeds])
    both = lax.all_gather(mine, "tp", axis=2, tiled=True)
    first_rows, given_rows = both[0], both[1]

    revised = jnp.where(accept[:, None] == 1, given_rows, first_rows)
    normed = normalize(jnp.concatenate([first_rows, revised], axis=0), norm_gain)
    normed5 = normed.reshape(normed.shape[0], n_ylo, n_z, 2, w_rows)
    normed5 = jnp.roll(normed5, -me_ylo, axis=1)
    normed5 = jnp.roll(normed5, -me_z, axis=2)
    normed5 = jnp.roll(normed5, -me_core, axis=3)
    line = jnp.stack([packed] + [shifted(packed, "ylo", n_ylo, k) for k in range(1, n_ylo)])
    arrived = [(0, line)]
    forward = line
    backward = line
    far = n_z // 2
    split = n_ylo // 2
    for step in range(1, far):
        forward = shifted(forward, "z", n_z, -1)
        backward = shifted(backward, "z", n_z, 1)
        arrived += [(-step, forward), (step, backward)]
    pair_index = lambda z, core: (z % n_z) * 2 + core
    to_partner_front = [(pair_index(z - 1, 1 - c), pair_index(z, c)) for z in range(n_z) for c in range(2)]
    to_partner_back = [(pair_index(z + 1, 1 - c), pair_index(z, c)) for z in range(n_z) for c in range(2)]
    far_own = jnp.concatenate(
        [shifted(forward[:split], "z", n_z, -1), shifted(backward[split:], "z", n_z, 1)], axis=0
    )
    far_other = jnp.concatenate(
        [
            lax.ppermute(forward[:split], ("z", "core"), to_partner_front),
            lax.ppermute(backward[split:], ("z", "core"), to_partner_back),
        ],
        axis=0,
    )
    normed5, far_own, far_other = lax.optimization_barrier((normed5, far_own, far_other))
    held = [(offset, 0, piece) for offset, piece in arrived]
    held += [(offset, 1, shifted(piece, "core", 2, 1)) for offset, piece in arrived]
    held += [(far, 0, far_own), (far, 1, far_other)]

    proj = None
    for offset, core, piece in held:
        part = jnp.einsum(
            "rki,kjid->rjd",
            normed5[:, :, offset % n_z, core, :],
            piece.reshape(n_ylo, total_blocks, w_rows, HD),
            preferred_element_type=jnp.float32,
        )
        proj = part if proj is None else proj + part
    queries = proj[:, : q_cols // HD, :].reshape(-1, q_cols) + b_query.astype(jnp.float32)
    key_proj = proj[:, q_cols // HD, :] + b_key.astype(jnp.float32)
    value_proj = proj[:, q_cols // HD + 1, :] + b_value.astype(jnp.float32)
    length = lengths[0]
    keep_row = block_keep[0]
    positions = length.astype(jnp.float32) + jnp.arange(block_rows, dtype=jnp.float32)
    q_rot = rotate(queries.reshape(2, block_rows, q_cols // HD, HD), positions).astype(jnp.bfloat16)
    k_rot = rotate(key_proj.reshape(2, block_rows, local_kv, HD), positions).astype(jnp.bfloat16)
    value_rows = value_proj.astype(jnp.bfloat16)

    blocks_all = keep_row.shape[0]
    cache_index = jnp.arange(blocks_all * ctx_rows, dtype=jnp.int32).reshape(n_ylo, n_z, 2, ctx_rows)
    kept = jnp.broadcast_to(keep_row.reshape(n_ylo, n_z, 2, 1), cache_index.shape) == 1
    visible = (cache_index < length) & kept
    bias4 = jnp.where(visible, 0.0, -jnp.inf).astype(jnp.float32)
    bias4 = jnp.roll(bias4, -me_ylo, axis=0)
    bias4 = jnp.roll(bias4, -me_z, axis=1)
    bias4 = jnp.roll(bias4, -me_core, axis=2)
    bias = jnp.concatenate([bias4[:, offset % n_z, core, :].reshape(1, -1) for offset, core, ignored in held], axis=1)
    cache_k = jnp.concatenate(
        [piece[:, key_start:value_start, :].reshape(-1, HD) for ignored, ignored2, piece in held], axis=0
    )
    cache_v = jnp.concatenate(
        [piece[:, value_start:used, :].reshape(-1, HD) for ignored, ignored2, piece in held], axis=0
    )
    attended = attend(
        q_rot.reshape(2, block_rows, q_cols),
        k_rot.reshape(2, block_rows, local_kv * HD),
        value_rows.reshape(2, block_rows, local_kv * HD),
        cache_k,
        cache_v,
        bias,
    )
    return (attended[0], attended[1])


def solution(mesh):
    blk_size, tp_size = mesh.devices.shape
    fine = Mesh(mesh.devices.reshape(4, blk_size // 8, 2, tp_size), ("ylo", "z", "core", "tp"))
    rows = ("ylo", "z", "core")
    return jax.shard_map(
        local,
        mesh=fine,
        in_specs=(
            P(rows, "tp"),
            P(rows, "tp"),
            P(rows),
            P(rows),
            P(rows, None),
            P(),
            P(rows, "tp"),
            P("tp"),
            P(rows, "tp"),
            P("tp"),
            P(rows, "tp"),
            P("tp"),
            P(rows, "tp"),
            P(rows, "tp"),
        ),
        out_specs=(P(rows, "tp"), P(rows, "tp")),
        check_vma=False,
    )
```

```python
import math

import jax
import jax.numpy as jnp
from jax import lax
from jax.experimental import pallas as pl
from jax.experimental.pallas import tpu as pltpu
from jax.sharding import Mesh
from jax.sharding import PartitionSpec as P

KVH = 8
HD = 128
HQ = 40
CB = 64


def rotate(vectors, positions):
    halfway = HD // 2
    frequency = 1000000.0 ** (-(jnp.arange(halfway, dtype=jnp.float32) * (2.0 / HD)))
    angles = positions[..., None] * frequency
    cosine = jnp.cos(angles)[..., None, :]
    sine_part = jnp.sin(angles)[..., None, :]
    front_part = vectors[..., :halfway]
    back_part = vectors[..., halfway:]
    return jnp.concatenate(
        [front_part * cosine - back_part * sine_part, back_part * cosine + front_part * sine_part],
        axis=-1,
    )


def normalize(rows_in, norm_gain):
    widened = rows_in.astype(jnp.float32)
    inverse = lax.rsqrt(jnp.mean(widened * widened, axis=-1, keepdims=True) + 1e-06)
    return (widened * inverse * norm_gain.astype(jnp.float32)).astype(jnp.bfloat16)


def attend_kernel(q_ref, ko_ref, vo_ref, kc_ref, vc_ref, bias_ref, out_ref):
    inv_root = 1.0 / math.sqrt(HD)
    q = q_ref[...]
    shards, ctx_rows, width = kc_ref.shape
    cache_k = kc_ref[...].reshape(shards * ctx_rows, width)
    cache_v = vc_ref[...].reshape(shards * ctx_rows, width)
    contract = (((1,), (1,)), ((), ()))
    own = lax.dot_general(q, ko_ref[...], contract, preferred_element_type=jnp.float32) * inv_root
    far = lax.dot_general(q, cache_k, contract, preferred_element_type=jnp.float32) * inv_root
    far = far + bias_ref[...]
    highest = jnp.maximum(jnp.max(own, axis=-1, keepdims=True), jnp.max(far, axis=-1, keepdims=True))
    own_w = jnp.exp(own - highest)
    far_w = jnp.exp(far - highest)
    totals = jnp.sum(own_w, axis=-1, keepdims=True) + jnp.sum(far_w, axis=-1, keepdims=True)
    mixture = jnp.dot(own_w.astype(jnp.bfloat16), vo_ref[...], preferred_element_type=jnp.float32)
    mixture = mixture + jnp.dot(far_w.astype(jnp.bfloat16), cache_v, preferred_element_type=jnp.float32)
    out_ref[...] = (mixture / totals).astype(out_ref.dtype)


def attend(q_rot, k_rot, value_rows, stacked, bias, key_block):
    passes, rows, width = q_rot.shape
    heads = width // HD
    ctx = bias.shape[1]
    shards = stacked.shape[0]
    ctx_rows = ctx // shards
    return pl.pallas_call(
        attend_kernel,
        grid=(passes, heads),
        in_specs=[
            pl.BlockSpec((None, rows, HD), lambda p, h: (p, 0, h)),
            pl.BlockSpec((None, rows, HD), lambda p, h: (p, 0, 0)),
            pl.BlockSpec((None, rows, HD), lambda p, h: (p, 0, 0)),
            pl.BlockSpec((shards, ctx_rows, HD), lambda p, h: (0, key_block, 0)),
            pl.BlockSpec((shards, ctx_rows, HD), lambda p, h: (0, key_block + 1, 0)),
            pl.BlockSpec((1, ctx), lambda p, h: (0, 0)),
        ],
        out_specs=pl.BlockSpec((None, rows, HD), lambda p, h: (p, 0, h)),
        out_shape=jax.ShapeDtypeStruct((passes, rows, width), jnp.bfloat16),
        cost_estimate=pl.CostEstimate(
            flops=4 * passes * heads * rows * (ctx + rows) * HD,
            transcendentals=passes * heads * rows * (ctx + rows),
            bytes_accessed=2 * (2 * ctx * HD + 4 * passes * rows * width),
        ),
    )(q_rot, k_rot, value_rows, stacked, stacked, bias)


def shifted(x, axis, size, shift):
    pairs = [(j, (j - shift) % size) for j in range(size)]
    return lax.ppermute(x, axis, pairs)


def local(
    embeds,
    given_embeds,
    accept,
    lengths,
    block_keep,
    norm_gain,
    w_query,
    b_query,
    w_key,
    b_key,
    w_value,
    b_value,
    cache_keys,
    cache_values,
):
    local_kv = w_key.shape[1] // HD
    block_rows = embeds.shape[0]
    ctx_rows = cache_keys.shape[0]
    q_cols = w_query.shape[1]
    w_rows = w_query.shape[0]

    w_parts = [w_query[:, j * HD : (j + 1) * HD] for j in range(q_cols // HD)] + [w_key, w_value]
    w_len = len(w_parts) * w_rows
    key_start = -(-w_len // ctx_rows) * ctx_rows
    value_start = key_start + ctx_rows
    used = value_start + ctx_rows
    total_blocks = -(-used // w_rows)
    lead = jnp.zeros((key_start - w_len, HD), w_query.dtype)
    tail = jnp.zeros((total_blocks * w_rows - used, HD), w_query.dtype)
    packed = jnp.concatenate(w_parts + [lead, cache_keys, cache_values, tail], axis=0)

    n_ylo = lax.axis_size("ylo")
    n_z = lax.axis_size("z")
    me_ylo = lax.axis_index("ylo")
    me_z = lax.axis_index("z")
    me_core = lax.axis_index("core")

    mine = jnp.stack([embeds, given_embeds])
    both = lax.all_gather(mine, "tp", axis=2, tiled=True)
    first_rows, given_rows = both[0], both[1]

    revised = jnp.where(accept[:, None] == 1, given_rows, first_rows)
    normed = normalize(jnp.concatenate([first_rows, revised], axis=0), norm_gain)
    normed5 = normed.reshape(normed.shape[0], n_ylo, n_z, 2, w_rows)
    normed5 = jnp.roll(normed5, -me_ylo, axis=1)
    normed5 = jnp.roll(normed5, -me_z, axis=2)
    normed5 = jnp.roll(normed5, -me_core, axis=3)
    line = jnp.stack([packed] + [shifted(packed, "ylo", n_ylo, k) for k in range(1, n_ylo)])
    arrived = [(0, line)]
    forward = line
    backward = line
    far = n_z // 2
    split = n_ylo // 2
    for step in range(1, far):
        forward = shifted(forward, "z", n_z, -1)
        backward = shifted(backward, "z", n_z, 1)
        arrived += [(-step, forward), (step, backward)]
    pair_index = lambda z, core: (z % n_z) * 2 + core
    to_partner_front = [(pair_index(z - 1, 1 - c), pair_index(z, c)) for z in range(n_z) for c in range(2)]
    to_partner_back = [(pair_index(z + 1, 1 - c), pair_index(z, c)) for z in range(n_z) for c in range(2)]
    far_own = jnp.concatenate(
        [shifted(forward[:split], "z", n_z, -1), shifted(backward[split:], "z", n_z, 1)], axis=0
    )
    far_other = jnp.concatenate(
        [
            lax.ppermute(forward[:split], ("z", "core"), to_partner_front),
            lax.ppermute(backward[split:], ("z", "core"), to_partner_back),
        ],
        axis=0,
    )
    normed5, far_own, far_other = lax.optimization_barrier((normed5, far_own, far_other))
    held = [(offset, 0, piece) for offset, piece in arrived]
    held += [(offset, 1, shifted(piece, "core", 2, 1)) for offset, piece in arrived]
    held += [(far, 0, far_own), (far, 1, far_other)]

    stacked = jnp.stack([piece for ignored, ignored2, piece in held])
    lhs = jnp.stack([normed5[:, :, offset % n_z, core, :] for offset, core, ignored in held], axis=1)
    proj = jnp.einsum(
        "rpki,pkjid->rjd",
        lhs,
        stacked.reshape(len(held), n_ylo, total_blocks, w_rows, HD),
        preferred_element_type=jnp.float32,
    )
    queries = proj[:, : q_cols // HD, :].reshape(-1, q_cols) + b_query.astype(jnp.float32)
    key_proj = proj[:, q_cols // HD, :] + b_key.astype(jnp.float32)
    value_proj = proj[:, q_cols // HD + 1, :] + b_value.astype(jnp.float32)
    length = lengths[0]
    keep_row = block_keep[0]
    positions = length.astype(jnp.float32) + jnp.arange(block_rows, dtype=jnp.float32)
    q_rot = rotate(queries.reshape(2, block_rows, q_cols // HD, HD), positions).astype(jnp.bfloat16)
    k_rot = rotate(key_proj.reshape(2, block_rows, local_kv, HD), positions).astype(jnp.bfloat16)
    value_rows = value_proj.astype(jnp.bfloat16)

    blocks_all = keep_row.shape[0]
    cache_index = jnp.arange(blocks_all * ctx_rows, dtype=jnp.int32).reshape(n_ylo, n_z, 2, ctx_rows)
    kept = jnp.broadcast_to(keep_row.reshape(n_ylo, n_z, 2, 1), cache_index.shape) == 1
    visible = (cache_index < length) & kept
    bias4 = jnp.where(visible, 0.0, -jnp.inf).astype(jnp.float32)
    bias4 = jnp.roll(bias4, -me_ylo, axis=0)
    bias4 = jnp.roll(bias4, -me_z, axis=1)
    bias4 = jnp.roll(bias4, -me_core, axis=2)
    bias = jnp.concatenate([bias4[:, offset % n_z, core, :].reshape(1, -1) for offset, core, ignored in held], axis=1)
    attended = attend(
        q_rot.reshape(2, block_rows, q_cols),
        k_rot.reshape(2, block_rows, local_kv * HD),
        value_rows.reshape(2, block_rows, local_kv * HD),
        stacked.reshape(-1, total_blocks * w_rows, HD),
        bias,
        key_start // ctx_rows,
    )
    return (attended[0], attended[1])


def solution(mesh):
    blk_size, tp_size = mesh.devices.shape
    fine = Mesh(mesh.devices.reshape(4, blk_size // 8, 2, tp_size), ("ylo", "z", "core", "tp"))
    rows = ("ylo", "z", "core")
    return jax.shard_map(
        local,
        mesh=fine,
        in_specs=(
            P(rows, "tp"),
            P(rows, "tp"),
            P(rows),
            P(rows),
            P(rows, None),
            P(),
            P(rows, "tp"),
            P("tp"),
            P(rows, "tp"),
            P("tp"),
            P(rows, "tp"),
            P("tp"),
            P(rows, "tp"),
            P(rows, "tp"),
        ),
        out_specs=(P(rows, "tp"), P(rows, "tp")),
        check_vma=False,
    )
```

```python
import math

import jax
import jax.numpy as jnp
from jax import lax
from jax.experimental import pallas as pl
from jax.experimental.pallas import tpu as pltpu
from jax.sharding import Mesh
from jax.sharding import PartitionSpec as P

KVH = 8
HD = 128
HQ = 40
CB = 64


def rotate(vectors, positions):
    halfway = HD // 2
    frequency = 1000000.0 ** (-(jnp.arange(halfway, dtype=jnp.float32) * (2.0 / HD)))
    angles = positions[..., None] * frequency
    cosine = jnp.cos(angles)[..., None, :]
    sine_part = jnp.sin(angles)[..., None, :]
    front_part = vectors[..., :halfway]
    back_part = vectors[..., halfway:]
    return jnp.concatenate(
        [front_part * cosine - back_part * sine_part, back_part * cosine + front_part * sine_part],
        axis=-1,
    )


def normalize(rows_in, norm_gain):
    widened = rows_in.astype(jnp.float32)
    inverse = lax.rsqrt(jnp.mean(widened * widened, axis=-1, keepdims=True) + 1e-06)
    return (widened * inverse * norm_gain.astype(jnp.float32)).astype(jnp.bfloat16)


def attend_kernel(q_ref, ko_ref, vo_ref, kc_ref, vc_ref, bias_ref, out_ref):
    inv_root = 1.0 / math.sqrt(HD)
    contract = (((1,), (1,)), ((), ()))
    own_keys = ko_ref[...]
    own_values = vo_ref[...]
    cache_k = kc_ref[...]
    cache_v = vc_ref[...]
    bias = bias_ref[...]
    for head in range(q_ref.shape[1] // HD):
        lanes = slice(head * HD, (head + 1) * HD)
        q = q_ref[:, lanes]
        own = lax.dot_general(q, own_keys, contract, preferred_element_type=jnp.float32) * inv_root
        far = lax.dot_general(q, cache_k, contract, preferred_element_type=jnp.float32) * inv_root
        far = far + bias
        highest = jnp.maximum(jnp.max(own, axis=-1, keepdims=True), jnp.max(far, axis=-1, keepdims=True))
        own_w = jnp.exp(own - highest)
        far_w = jnp.exp(far - highest)
        totals = jnp.sum(own_w, axis=-1, keepdims=True) + jnp.sum(far_w, axis=-1, keepdims=True)
        mixture = jnp.dot(own_w.astype(jnp.bfloat16), own_values, preferred_element_type=jnp.float32)
        mixture = mixture + jnp.dot(far_w.astype(jnp.bfloat16), cache_v, preferred_element_type=jnp.float32)
        out_ref[:, lanes] = (mixture / totals).astype(out_ref.dtype)


def attend(q_rot, k_rot, value_rows, cache_k, cache_v, bias):
    passes, rows, width = q_rot.shape
    heads = width // HD
    ctx = cache_k.shape[0]
    return pl.pallas_call(
        attend_kernel,
        grid=(passes,),
        in_specs=[
            pl.BlockSpec((None, rows, width), lambda p: (p, 0, 0)),
            pl.BlockSpec((None, rows, HD), lambda p: (p, 0, 0)),
            pl.BlockSpec((None, rows, HD), lambda p: (p, 0, 0)),
            pl.BlockSpec((ctx, HD), lambda p: (0, 0)),
            pl.BlockSpec((ctx, HD), lambda p: (0, 0)),
            pl.BlockSpec((1, ctx), lambda p: (0, 0)),
        ],
        out_specs=pl.BlockSpec((None, rows, width), lambda p: (p, 0, 0)),
        out_shape=jax.ShapeDtypeStruct((passes, rows, width), jnp.bfloat16),
        cost_estimate=pl.CostEstimate(
            flops=4 * passes * heads * rows * (ctx + rows) * HD,
            transcendentals=passes * heads * rows * (ctx + rows),
            bytes_accessed=2 * (2 * ctx * HD + 4 * passes * rows * width),
        ),
    )(q_rot, k_rot, value_rows, cache_k, cache_v, bias)


def shifted(x, axis, size, shift):
    pairs = [(j, (j - shift) % size) for j in range(size)]
    return lax.ppermute(x, axis, pairs)


def local(
    embeds,
    given_embeds,
    accept,
    lengths,
    block_keep,
    norm_gain,
    w_query,
    b_query,
    w_key,
    b_key,
    w_value,
    b_value,
    cache_keys,
    cache_values,
):
    local_kv = w_key.shape[1] // HD
    block_rows = embeds.shape[0]
    ctx_rows = cache_keys.shape[0]
    q_cols = w_query.shape[1]
    w_rows = w_query.shape[0]

    w_parts = [w_query[:, j * HD : (j + 1) * HD] for j in range(q_cols // HD)] + [w_key, w_value]
    w_len = len(w_parts) * w_rows
    key_start = -(-w_len // ctx_rows) * ctx_rows
    value_start = key_start + ctx_rows
    used = value_start + ctx_rows
    total_blocks = -(-used // w_rows)
    lead = jnp.zeros((key_start - w_len, HD), w_query.dtype)
    tail = jnp.zeros((total_blocks * w_rows - used, HD), w_query.dtype)
    packed = jnp.concatenate(w_parts + [lead, cache_keys, cache_values, tail], axis=0)

    n_ylo = lax.axis_size("ylo")
    n_z = lax.axis_size("z")
    me_ylo = lax.axis_index("ylo")
    me_z = lax.axis_index("z")
    me_core = lax.axis_index("core")

    mine = jnp.stack([embeds, given_embeds])
    both = lax.all_gather(mine, "tp", axis=2, tiled=True)
    first_rows, given_rows = both[0], both[1]

    revised = jnp.where(accept[:, None] == 1, given_rows, first_rows)
    normed = normalize(jnp.concatenate([first_rows, revised], axis=0), norm_gain)
    normed5 = normed.reshape(normed.shape[0], n_ylo, n_z, 2, w_rows)
    normed5 = jnp.roll(normed5, -me_ylo, axis=1)
    normed5 = jnp.roll(normed5, -me_z, axis=2)
    normed5 = jnp.roll(normed5, -me_core, axis=3)
    line = jnp.stack([packed] + [shifted(packed, "ylo", n_ylo, k) for k in range(1, n_ylo)])
    arrived = [(0, line)]
    forward = line
    backward = line
    far = n_z // 2
    split = n_ylo // 2
    for step in range(1, far):
        forward = shifted(forward, "z", n_z, -1)
        backward = shifted(backward, "z", n_z, 1)
        arrived += [(-step, forward), (step, backward)]
    pair_index = lambda z, core: (z % n_z) * 2 + core
    to_partner_front = [(pair_index(z - 1, 1 - c), pair_index(z, c)) for z in range(n_z) for c in range(2)]
    to_partner_back = [(pair_index(z + 1, 1 - c), pair_index(z, c)) for z in range(n_z) for c in range(2)]
    far_own = jnp.concatenate(
        [shifted(forward[:split], "z", n_z, -1), shifted(backward[split:], "z", n_z, 1)], axis=0
    )
    far_other = jnp.concatenate(
        [
            lax.ppermute(forward[:split], ("z", "core"), to_partner_front),
            lax.ppermute(backward[split:], ("z", "core"), to_partner_back),
        ],
        axis=0,
    )
    normed5, far_own, far_other = lax.optimization_barrier((normed5, far_own, far_other))
    held = [(offset, 0, piece) for offset, piece in arrived]
    held += [(offset, 1, shifted(piece, "core", 2, 1)) for offset, piece in arrived]
    held += [(far, 0, far_own), (far, 1, far_other)]

    proj = None
    for offset, core, piece in held:
        part = jnp.einsum(
            "rki,kjid->rjd",
            normed5[:, :, offset % n_z, core, :],
            piece.reshape(n_ylo, total_blocks, w_rows, HD),
            preferred_element_type=jnp.float32,
        )
        proj = part if proj is None else proj + part
    queries = proj[:, : q_cols // HD, :].reshape(-1, q_cols) + b_query.astype(jnp.float32)
    key_proj = proj[:, q_cols // HD, :] + b_key.astype(jnp.float32)
    value_proj = proj[:, q_cols // HD + 1, :] + b_value.astype(jnp.float32)
    length = lengths[0]
    keep_row = block_keep[0]
    positions = length.astype(jnp.float32) + jnp.arange(block_rows, dtype=jnp.float32)
    q_rot = rotate(queries.reshape(2, block_rows, q_cols // HD, HD), positions).astype(jnp.bfloat16)
    k_rot = rotate(key_proj.reshape(2, block_rows, local_kv, HD), positions).astype(jnp.bfloat16)
    value_rows = value_proj.astype(jnp.bfloat16)

    blocks_all = keep_row.shape[0]
    cache_index = jnp.arange(blocks_all * ctx_rows, dtype=jnp.int32).reshape(n_ylo, n_z, 2, ctx_rows)
    kept = jnp.broadcast_to(keep_row.reshape(n_ylo, n_z, 2, 1), cache_index.shape) == 1
    visible = (cache_index < length) & kept
    bias4 = jnp.where(visible, 0.0, -jnp.inf).astype(jnp.float32)
    bias4 = jnp.roll(bias4, -me_ylo, axis=0)
    bias4 = jnp.roll(bias4, -me_z, axis=1)
    bias4 = jnp.roll(bias4, -me_core, axis=2)
    bias = jnp.concatenate([bias4[:, offset % n_z, core, :].reshape(1, -1) for offset, core, ignored in held], axis=1)
    cache_k = jnp.concatenate(
        [piece[:, key_start:value_start, :].reshape(-1, HD) for ignored, ignored2, piece in held], axis=0
    )
    cache_v = jnp.concatenate(
        [piece[:, value_start:used, :].reshape(-1, HD) for ignored, ignored2, piece in held], axis=0
    )
    attended = attend(
        q_rot.reshape(2, block_rows, q_cols),
        k_rot.reshape(2, block_rows, local_kv * HD),
        value_rows.reshape(2, block_rows, local_kv * HD),
        cache_k,
        cache_v,
        bias,
    )
    return (attended[0], attended[1])


def solution(mesh):
    blk_size, tp_size = mesh.devices.shape
    fine = Mesh(mesh.devices.reshape(4, blk_size // 8, 2, tp_size), ("ylo", "z", "core", "tp"))
    rows = ("ylo", "z", "core")
    return jax.shard_map(
        local,
        mesh=fine,
        in_specs=(
            P(rows, "tp"),
            P(rows, "tp"),
            P(rows),
            P(rows),
            P(rows, None),
            P(),
            P(rows, "tp"),
            P("tp"),
            P(rows, "tp"),
            P("tp"),
            P(rows, "tp"),
            P("tp"),
            P(rows, "tp"),
            P(rows, "tp"),
        ),
        out_specs=(P(rows, "tp"), P(rows, "tp")),
        check_vma=False,
    )
```

```python
import math

import jax
import jax.numpy as jnp
from jax import lax
from jax.experimental import pallas as pl
from jax.experimental.pallas import tpu as pltpu
from jax.sharding import Mesh
from jax.sharding import PartitionSpec as P

KVH = 8
HD = 128
HQ = 40
CB = 64


def rotate(vectors, positions):
    halfway = HD // 2
    frequency = 1000000.0 ** (-(jnp.arange(halfway, dtype=jnp.float32) * (2.0 / HD)))
    angles = positions[..., None] * frequency
    cosine = jnp.cos(angles)[..., None, :]
    sine_part = jnp.sin(angles)[..., None, :]
    front_part = vectors[..., :halfway]
    back_part = vectors[..., halfway:]
    return jnp.concatenate(
        [front_part * cosine - back_part * sine_part, back_part * cosine + front_part * sine_part],
        axis=-1,
    )


def normalize(rows_in, norm_gain):
    widened = rows_in.astype(jnp.float32)
    inverse = lax.rsqrt(jnp.mean(widened * widened, axis=-1, keepdims=True) + 1e-06)
    return (widened * inverse * norm_gain.astype(jnp.float32)).astype(jnp.bfloat16)


def attend_kernel(q_ref, ko_ref, vo_ref, kc_ref, vc_ref, bias_ref, out_ref):
    inv_root = 1.0 / math.sqrt(HD)
    contract = (((1,), (1,)), ((), ()))
    own_keys = ko_ref[...]
    own_values = vo_ref[...]
    cache_k = kc_ref[...]
    cache_v = vc_ref[...]
    bias = bias_ref[...]
    for head in range(q_ref.shape[1] // HD):
        lanes = slice(head * HD, (head + 1) * HD)
        q = q_ref[:, lanes]
        own = lax.dot_general(q, own_keys, contract, preferred_element_type=jnp.float32) * inv_root
        far = lax.dot_general(q, cache_k, contract, preferred_element_type=jnp.float32) * inv_root
        far = far + bias
        highest = jnp.maximum(jnp.max(own, axis=-1, keepdims=True), jnp.max(far, axis=-1, keepdims=True))
        own_w = jnp.exp(own - highest)
        far_w = jnp.exp(far - highest)
        totals = jnp.sum(own_w, axis=-1, keepdims=True) + jnp.sum(far_w, axis=-1, keepdims=True)
        mixture = jnp.dot(own_w.astype(jnp.bfloat16), own_values, preferred_element_type=jnp.float32)
        mixture = mixture + jnp.dot(far_w.astype(jnp.bfloat16), cache_v, preferred_element_type=jnp.float32)
        out_ref[:, lanes] = (mixture / totals).astype(out_ref.dtype)


def attend(q_rot, k_rot, value_rows, cache_k, cache_v, bias):
    passes, rows, width = q_rot.shape
    heads = width // HD
    ctx = cache_k.shape[0]
    return pl.pallas_call(
        attend_kernel,
        grid=(passes,),
        in_specs=[
            pl.BlockSpec((None, rows, width), lambda p: (p, 0, 0)),
            pl.BlockSpec((None, rows, HD), lambda p: (p, 0, 0)),
            pl.BlockSpec((None, rows, HD), lambda p: (p, 0, 0)),
            pl.BlockSpec((ctx, HD), lambda p: (0, 0)),
            pl.BlockSpec((ctx, HD), lambda p: (0, 0)),
            pl.BlockSpec((1, ctx), lambda p: (0, 0)),
        ],
        out_specs=pl.BlockSpec((None, rows, width), lambda p: (p, 0, 0)),
        out_shape=jax.ShapeDtypeStruct((passes, rows, width), jnp.bfloat16),
        cost_estimate=pl.CostEstimate(
            flops=4 * passes * heads * rows * (ctx + rows) * HD,
            transcendentals=passes * heads * rows * (ctx + rows),
            bytes_accessed=2 * (2 * ctx * HD + 4 * passes * rows * width),
        ),
    )(q_rot, k_rot, value_rows, cache_k, cache_v, bias)


def shifted(x, axis, size, shift):
    pairs = [(j, (j - shift) % size) for j in range(size)]
    return lax.ppermute(x, axis, pairs)


def local(
    embeds,
    given_embeds,
    accept,
    lengths,
    block_keep,
    norm_gain,
    w_query,
    b_query,
    w_key,
    b_key,
    w_value,
    b_value,
    cache_keys,
    cache_values,
):
    local_kv = w_key.shape[1] // HD
    block_rows = embeds.shape[0]
    ctx_rows = cache_keys.shape[0]
    q_cols = w_query.shape[1]
    w_rows = w_query.shape[0]

    w_parts = [w_query[:, j * HD : (j + 1) * HD] for j in range(q_cols // HD)] + [w_key, w_value]
    w_len = len(w_parts) * w_rows
    key_start = -(-w_len // ctx_rows) * ctx_rows
    value_start = key_start + ctx_rows
    used = value_start + ctx_rows
    total_blocks = -(-used // w_rows)
    lead = jnp.zeros((key_start - w_len, HD), w_query.dtype)
    tail = jnp.zeros((total_blocks * w_rows - used, HD), w_query.dtype)
    packed = jnp.concatenate(w_parts + [lead, cache_keys, cache_values, tail], axis=0)

    n_ylo = lax.axis_size("ylo")
    n_z = lax.axis_size("z")
    me_ylo = lax.axis_index("ylo")
    me_z = lax.axis_index("z")
    me_core = lax.axis_index("core")

    mine = jnp.stack([embeds, given_embeds])
    me_yhi = lax.axis_index("yhi")
    pair = jnp.roll(jnp.stack([mine, shifted(mine, "yhi", 2, 1)]), me_yhi, axis=0)
    spread = lax.all_gather(pair, "x", axis=1, tiled=False)
    both = jnp.transpose(spread, (2, 3, 0, 1, 4)).reshape(mine.shape[0], mine.shape[1], -1)
    first_rows, given_rows = both[0], both[1]

    revised = jnp.where(accept[:, None] == 1, given_rows, first_rows)
    normed = normalize(jnp.concatenate([first_rows, revised], axis=0), norm_gain)
    normed5 = normed.reshape(normed.shape[0], n_ylo, n_z, 2, w_rows)
    normed5 = jnp.roll(normed5, -me_ylo, axis=1)
    normed5 = jnp.roll(normed5, -me_z, axis=2)
    normed5 = jnp.roll(normed5, -me_core, axis=3)
    line = jnp.stack([packed] + [shifted(packed, "ylo", n_ylo, k) for k in range(1, n_ylo)])
    arrived = [(0, line)]
    forward = line
    backward = line
    far = n_z // 2
    split = n_ylo // 2
    for step in range(1, far):
        if step == far - 1:
            normed5, forward, backward = lax.optimization_barrier((normed5, forward, backward))
        forward = shifted(forward, "z", n_z, -1)
        backward = shifted(backward, "z", n_z, 1)
        arrived += [(-step, forward), (step, backward)]
    pair_index = lambda z, core: (z % n_z) * 2 + core
    to_partner_front = [(pair_index(z - 1, 1 - c), pair_index(z, c)) for z in range(n_z) for c in range(2)]
    to_partner_back = [(pair_index(z + 1, 1 - c), pair_index(z, c)) for z in range(n_z) for c in range(2)]
    far_own = jnp.concatenate(
        [shifted(forward[:split], "z", n_z, -1), shifted(backward[split:], "z", n_z, 1)], axis=0
    )
    far_other = jnp.concatenate(
        [
            lax.ppermute(forward[:split], ("z", "core"), to_partner_front),
            lax.ppermute(backward[split:], ("z", "core"), to_partner_back),
        ],
        axis=0,
    )
    held = [(offset, 0, piece) for offset, piece in arrived]
    held += [(offset, 1, shifted(piece, "core", 2, 1)) for offset, piece in arrived]
    held += [(far, 0, far_own), (far, 1, far_other)]

    proj = None
    for offset, core, piece in held:
        part = jnp.einsum(
            "rki,kjid->rjd",
            normed5[:, :, offset % n_z, core, :],
            piece.reshape(n_ylo, total_blocks, w_rows, HD),
            preferred_element_type=jnp.float32,
        )
        proj = part if proj is None else proj + part
    queries = proj[:, : q_cols // HD, :].reshape(-1, q_cols) + b_query.astype(jnp.float32)
    key_proj = proj[:, q_cols // HD, :] + b_key.astype(jnp.float32)
    value_proj = proj[:, q_cols // HD + 1, :] + b_value.astype(jnp.float32)
    length = lengths[0]
    keep_row = block_keep[0]
    positions = length.astype(jnp.float32) + jnp.arange(block_rows, dtype=jnp.float32)
    q_rot = rotate(queries.reshape(2, block_rows, q_cols // HD, HD), positions).astype(jnp.bfloat16)
    k_rot = rotate(key_proj.reshape(2, block_rows, local_kv, HD), positions).astype(jnp.bfloat16)
    value_rows = value_proj.astype(jnp.bfloat16)

    blocks_all = keep_row.shape[0]
    cache_index = jnp.arange(blocks_all * ctx_rows, dtype=jnp.int32).reshape(n_ylo, n_z, 2, ctx_rows)
    kept = jnp.broadcast_to(keep_row.reshape(n_ylo, n_z, 2, 1), cache_index.shape) == 1
    visible = (cache_index < length) & kept
    bias4 = jnp.where(visible, 0.0, -jnp.inf).astype(jnp.float32)
    bias4 = jnp.roll(bias4, -me_ylo, axis=0)
    bias4 = jnp.roll(bias4, -me_z, axis=1)
    bias4 = jnp.roll(bias4, -me_core, axis=2)
    bias = jnp.concatenate([bias4[:, offset % n_z, core, :].reshape(1, -1) for offset, core, ignored in held], axis=1)
    cache_k = jnp.concatenate(
        [piece[:, key_start:value_start, :].reshape(-1, HD) for ignored, ignored2, piece in held], axis=0
    )
    cache_v = jnp.concatenate(
        [piece[:, value_start:used, :].reshape(-1, HD) for ignored, ignored2, piece in held], axis=0
    )
    attended = attend(
        q_rot.reshape(2, block_rows, q_cols),
        k_rot.reshape(2, block_rows, local_kv * HD),
        value_rows.reshape(2, block_rows, local_kv * HD),
        cache_k,
        cache_v,
        bias,
    )
    return (attended[0], attended[1])


def solution(mesh):
    blk_size, tp_size = mesh.devices.shape
    fine = Mesh(mesh.devices.reshape(4, blk_size // 8, 2, 2, tp_size // 2), ("ylo", "z", "core", "yhi", "x"))
    rows = ("ylo", "z", "core")
    cols = ("yhi", "x")
    return jax.shard_map(
        local,
        mesh=fine,
        in_specs=(
            P(rows, cols),
            P(rows, cols),
            P(rows),
            P(rows),
            P(rows, None),
            P(),
            P(rows, cols),
            P(cols),
            P(rows, cols),
            P(cols),
            P(rows, cols),
            P(cols),
            P(rows, cols),
            P(rows, cols),
        ),
        out_specs=(P(rows, cols), P(rows, cols)),
        check_vma=False,
    )
```

```python
import math

import jax
import jax.numpy as jnp
from jax import lax
from jax.experimental import pallas as pl
from jax.experimental.pallas import tpu as pltpu
from jax.sharding import Mesh
from jax.sharding import PartitionSpec as P

KVH = 8
HD = 128
HQ = 40
CB = 64


def rotate(vectors, positions):
    halfway = HD // 2
    frequency = 1000000.0 ** (-(jnp.arange(halfway, dtype=jnp.float32) * (2.0 / HD)))
    angles = positions[..., None] * frequency
    cosine = jnp.cos(angles)[..., None, :]
    sine_part = jnp.sin(angles)[..., None, :]
    front_part = vectors[..., :halfway]
    back_part = vectors[..., halfway:]
    return jnp.concatenate(
        [front_part * cosine - back_part * sine_part, back_part * cosine + front_part * sine_part],
        axis=-1,
    )


def normalize(rows_in, norm_gain):
    widened = rows_in.astype(jnp.float32)
    inverse = lax.rsqrt(jnp.mean(widened * widened, axis=-1, keepdims=True) + 1e-06)
    return (widened * inverse * norm_gain.astype(jnp.float32)).astype(jnp.bfloat16)


def attend_kernel(q_ref, ko_ref, vo_ref, kc_ref, vc_ref, bias_ref, out_ref):
    inv_root = 1.0 / math.sqrt(HD)
    contract = (((1,), (1,)), ((), ()))
    own_keys = ko_ref[...]
    own_values = vo_ref[...]
    cache_k = kc_ref[...]
    cache_v = vc_ref[...]
    bias = bias_ref[...]
    for head in range(q_ref.shape[1] // HD):
        lanes = slice(head * HD, (head + 1) * HD)
        q = q_ref[:, lanes]
        own = lax.dot_general(q, own_keys, contract, preferred_element_type=jnp.float32) * inv_root
        far = lax.dot_general(q, cache_k, contract, preferred_element_type=jnp.float32) * inv_root
        far = far + bias
        highest = jnp.maximum(jnp.max(own, axis=-1, keepdims=True), jnp.max(far, axis=-1, keepdims=True))
        own_w = jnp.exp(own - highest)
        far_w = jnp.exp(far - highest)
        totals = jnp.sum(own_w, axis=-1, keepdims=True) + jnp.sum(far_w, axis=-1, keepdims=True)
        mixture = jnp.dot(own_w.astype(jnp.bfloat16), own_values, preferred_element_type=jnp.float32)
        mixture = mixture + jnp.dot(far_w.astype(jnp.bfloat16), cache_v, preferred_element_type=jnp.float32)
        out_ref[:, lanes] = (mixture / totals).astype(out_ref.dtype)


def attend(q_rot, k_rot, value_rows, cache_k, cache_v, bias):
    passes, rows, width = q_rot.shape
    heads = width // HD
    ctx = cache_k.shape[0]
    return pl.pallas_call(
        attend_kernel,
        grid=(passes,),
        in_specs=[
            pl.BlockSpec((None, rows, width), lambda p: (p, 0, 0)),
            pl.BlockSpec((None, rows, HD), lambda p: (p, 0, 0)),
            pl.BlockSpec((None, rows, HD), lambda p: (p, 0, 0)),
            pl.BlockSpec((ctx, HD), lambda p: (0, 0)),
            pl.BlockSpec((ctx, HD), lambda p: (0, 0)),
            pl.BlockSpec((1, ctx), lambda p: (0, 0)),
        ],
        out_specs=pl.BlockSpec((None, rows, width), lambda p: (p, 0, 0)),
        out_shape=jax.ShapeDtypeStruct((passes, rows, width), jnp.bfloat16),
        cost_estimate=pl.CostEstimate(
            flops=4 * passes * heads * rows * (ctx + rows) * HD,
            transcendentals=passes * heads * rows * (ctx + rows),
            bytes_accessed=2 * (2 * ctx * HD + 4 * passes * rows * width),
        ),
    )(q_rot, k_rot, value_rows, cache_k, cache_v, bias)


def shifted(x, axis, size, shift):
    pairs = [(j, (j - shift) % size) for j in range(size)]
    return lax.ppermute(x, axis, pairs)


def local(
    embeds,
    given_embeds,
    accept,
    lengths,
    block_keep,
    norm_gain,
    w_query,
    b_query,
    w_key,
    b_key,
    w_value,
    b_value,
    cache_keys,
    cache_values,
):
    local_kv = w_key.shape[1] // HD
    block_rows = embeds.shape[0]
    ctx_rows = cache_keys.shape[0]
    q_cols = w_query.shape[1]
    w_rows = w_query.shape[0]

    w_parts = [w_query[:, j * HD : (j + 1) * HD] for j in range(q_cols // HD)] + [w_key, w_value]
    w_len = len(w_parts) * w_rows
    key_start = -(-w_len // ctx_rows) * ctx_rows
    value_start = key_start + ctx_rows
    used = value_start + ctx_rows
    total_blocks = -(-used // w_rows)
    lead = jnp.zeros((key_start - w_len, HD), w_query.dtype)
    tail = jnp.zeros((total_blocks * w_rows - used, HD), w_query.dtype)
    packed = jnp.concatenate(w_parts + [lead, cache_keys, cache_values, tail], axis=0)

    n_ylo = lax.axis_size("ylo")
    n_z = lax.axis_size("z")
    me_ylo = lax.axis_index("ylo")
    me_z = lax.axis_index("z")
    me_core = lax.axis_index("core")

    mine = jnp.stack([embeds, given_embeds])
    me_yhi = lax.axis_index("yhi")
    pair = jnp.roll(jnp.stack([mine, shifted(mine, "yhi", 2, 1)]), me_yhi, axis=0)
    spread = lax.all_gather(pair, "x", axis=1, tiled=False)
    both = jnp.transpose(spread, (2, 3, 0, 1, 4)).reshape(mine.shape[0], mine.shape[1], -1)
    first_rows, given_rows = both[0], both[1]

    revised = jnp.where(accept[:, None] == 1, given_rows, first_rows)
    normed = normalize(jnp.concatenate([first_rows, revised], axis=0), norm_gain)
    normed5 = normed.reshape(normed.shape[0], n_ylo, n_z, 2, w_rows)
    normed5 = jnp.roll(normed5, -me_ylo, axis=1)
    normed5 = jnp.roll(normed5, -me_z, axis=2)
    normed5 = jnp.roll(normed5, -me_core, axis=3)
    line = jnp.stack([packed] + [shifted(packed, "ylo", n_ylo, k) for k in range(1, n_ylo)])
    arrived = [(0, line)]
    forward = line
    backward = line
    far = n_z // 2
    split = n_ylo // 2
    for step in range(1, far):
        forward = shifted(forward, "z", n_z, -1)
        backward = shifted(backward, "z", n_z, 1)
        arrived += [(-step, forward), (step, backward)]
    pair_index = lambda z, core: (z % n_z) * 2 + core
    to_partner_front = [(pair_index(z - 1, 1 - c), pair_index(z, c)) for z in range(n_z) for c in range(2)]
    to_partner_back = [(pair_index(z + 1, 1 - c), pair_index(z, c)) for z in range(n_z) for c in range(2)]
    far_own = jnp.concatenate(
        [shifted(forward[:split], "z", n_z, -1), shifted(backward[split:], "z", n_z, 1)], axis=0
    )
    far_other = jnp.concatenate(
        [
            lax.ppermute(forward[:split], ("z", "core"), to_partner_front),
            lax.ppermute(backward[split:], ("z", "core"), to_partner_back),
        ],
        axis=0,
    )
    normed5, far_own, far_other = lax.optimization_barrier((normed5, far_own, far_other))
    held = [(offset, 0, piece) for offset, piece in arrived]
    held += [(offset, 1, shifted(piece, "core", 2, 1)) for offset, piece in arrived]
    held += [(far, 0, far_own), (far, 1, far_other)]

    proj = None
    for offset, core, piece in held:
        part = jnp.einsum(
            "rki,kjid->rjd",
            normed5[:, :, offset % n_z, core, :],
            piece.reshape(n_ylo, total_blocks, w_rows, HD),
            preferred_element_type=jnp.float32,
        )
        proj = part if proj is None else proj + part
    queries = proj[:, : q_cols // HD, :].reshape(-1, q_cols) + b_query.astype(jnp.float32)
    key_proj = proj[:, q_cols // HD, :] + b_key.astype(jnp.float32)
    value_proj = proj[:, q_cols // HD + 1, :] + b_value.astype(jnp.float32)
    length = lengths[0]
    keep_row = block_keep[0]
    positions = length.astype(jnp.float32) + jnp.arange(block_rows, dtype=jnp.float32)
    q_rot = rotate(queries.reshape(2, block_rows, q_cols // HD, HD), positions).astype(jnp.bfloat16)
    k_rot = rotate(key_proj.reshape(2, block_rows, local_kv, HD), positions).astype(jnp.bfloat16)
    value_rows = value_proj.astype(jnp.bfloat16)

    blocks_all = keep_row.shape[0]
    cache_index = jnp.arange(blocks_all * ctx_rows, dtype=jnp.int32).reshape(n_ylo, n_z, 2, ctx_rows)
    kept = jnp.broadcast_to(keep_row.reshape(n_ylo, n_z, 2, 1), cache_index.shape) == 1
    visible = (cache_index < length) & kept
    bias4 = jnp.where(visible, 0.0, -jnp.inf).astype(jnp.float32)
    bias4 = jnp.roll(bias4, -me_ylo, axis=0)
    bias4 = jnp.roll(bias4, -me_z, axis=1)
    bias4 = jnp.roll(bias4, -me_core, axis=2)
    bias = jnp.concatenate([bias4[:, offset % n_z, core, :].reshape(1, -1) for offset, core, ignored in held], axis=1)
    cache_k = jnp.concatenate(
        [piece[:, key_start:value_start, :].reshape(-1, HD) for ignored, ignored2, piece in held], axis=0
    )
    cache_v = jnp.concatenate(
        [piece[:, value_start:used, :].reshape(-1, HD) for ignored, ignored2, piece in held], axis=0
    )
    attended = attend(
        q_rot.reshape(2, block_rows, q_cols),
        k_rot.reshape(2, block_rows, local_kv * HD),
        value_rows.reshape(2, block_rows, local_kv * HD),
        cache_k,
        cache_v,
        bias,
    )
    return (attended[0], attended[1])


def solution(mesh):
    blk_size, tp_size = mesh.devices.shape
    fine = Mesh(mesh.devices.reshape(4, blk_size // 8, 2, 2, tp_size // 2), ("ylo", "z", "core", "yhi", "x"))
    rows = ("ylo", "z", "core")
    cols = ("yhi", "x")
    return jax.shard_map(
        local,
        mesh=fine,
        in_specs=(
            P(rows, cols),
            P(rows, cols),
            P(rows),
            P(rows),
            P(rows, None),
            P(),
            P(rows, cols),
            P(cols),
            P(rows, cols),
            P(cols),
            P(rows, cols),
            P(cols),
            P(rows, cols),
            P(rows, cols),
        ),
        out_specs=(P(rows, cols), P(rows, cols)),
        check_vma=False,
    )
```

```python
import math

import jax
import jax.numpy as jnp
from jax import lax
from jax.experimental import pallas as pl
from jax.experimental.pallas import tpu as pltpu
from jax.sharding import Mesh
from jax.sharding import PartitionSpec as P

KVH = 8
HD = 128
HQ = 40
CB = 64


def rotate(vectors, positions):
    halfway = HD // 2
    frequency = 1000000.0 ** (-(jnp.arange(halfway, dtype=jnp.float32) * (2.0 / HD)))
    angles = positions[..., None] * frequency
    cosine = jnp.cos(angles)[..., None, :]
    sine_part = jnp.sin(angles)[..., None, :]
    front_part = vectors[..., :halfway]
    back_part = vectors[..., halfway:]
    return jnp.concatenate(
        [front_part * cosine - back_part * sine_part, back_part * cosine + front_part * sine_part],
        axis=-1,
    )


def normalize(rows_in, norm_gain):
    widened = rows_in.astype(jnp.float32)
    inverse = lax.rsqrt(jnp.mean(widened * widened, axis=-1, keepdims=True) + 1e-06)
    return (widened * inverse * norm_gain.astype(jnp.float32)).astype(jnp.bfloat16)


def attend_kernel(q_ref, ko_ref, vo_ref, kc_ref, vc_ref, bias_ref, out_ref):
    inv_root = 1.0 / math.sqrt(HD)
    contract = (((1,), (1,)), ((), ()))
    own_keys = ko_ref[...]
    own_values = vo_ref[...]
    cache_k = kc_ref[...]
    cache_v = vc_ref[...]
    bias = bias_ref[...]
    for head in range(q_ref.shape[1] // HD):
        lanes = slice(head * HD, (head + 1) * HD)
        q = q_ref[:, lanes]
        own = lax.dot_general(q, own_keys, contract, preferred_element_type=jnp.float32) * inv_root
        far = lax.dot_general(q, cache_k, contract, preferred_element_type=jnp.float32) * inv_root
        far = far + bias
        highest = jnp.maximum(jnp.max(own, axis=-1, keepdims=True), jnp.max(far, axis=-1, keepdims=True))
        own_w = jnp.exp(own - highest)
        far_w = jnp.exp(far - highest)
        totals = jnp.sum(own_w, axis=-1, keepdims=True) + jnp.sum(far_w, axis=-1, keepdims=True)
        mixture = jnp.dot(own_w.astype(jnp.bfloat16), own_values, preferred_element_type=jnp.float32)
        mixture = mixture + jnp.dot(far_w.astype(jnp.bfloat16), cache_v, preferred_element_type=jnp.float32)
        out_ref[:, lanes] = (mixture / totals).astype(out_ref.dtype)


def attend(q_rot, k_rot, value_rows, cache_k, cache_v, bias):
    passes, rows, width = q_rot.shape
    heads = width // HD
    ctx = cache_k.shape[0]
    return pl.pallas_call(
        attend_kernel,
        grid=(passes,),
        in_specs=[
            pl.BlockSpec((None, rows, width), lambda p: (p, 0, 0)),
            pl.BlockSpec((None, rows, HD), lambda p: (p, 0, 0)),
            pl.BlockSpec((None, rows, HD), lambda p: (p, 0, 0)),
            pl.BlockSpec((ctx, HD), lambda p: (0, 0)),
            pl.BlockSpec((ctx, HD), lambda p: (0, 0)),
            pl.BlockSpec((1, ctx), lambda p: (0, 0)),
        ],
        out_specs=pl.BlockSpec((None, rows, width), lambda p: (p, 0, 0)),
        out_shape=jax.ShapeDtypeStruct((passes, rows, width), jnp.bfloat16),
        cost_estimate=pl.CostEstimate(
            flops=4 * passes * heads * rows * (ctx + rows) * HD,
            transcendentals=passes * heads * rows * (ctx + rows),
            bytes_accessed=2 * (2 * ctx * HD + 4 * passes * rows * width),
        ),
    )(q_rot, k_rot, value_rows, cache_k, cache_v, bias)


def shifted(x, axis, size, shift):
    pairs = [(j, (j - shift) % size) for j in range(size)]
    return lax.ppermute(x, axis, pairs)


def local(
    embeds,
    given_embeds,
    accept,
    lengths,
    block_keep,
    norm_gain,
    w_query,
    b_query,
    w_key,
    b_key,
    w_value,
    b_value,
    cache_keys,
    cache_values,
):
    local_kv = w_key.shape[1] // HD
    block_rows = embeds.shape[0]
    ctx_rows = cache_keys.shape[0]
    q_cols = w_query.shape[1]
    w_rows = w_query.shape[0]

    mine = jnp.stack([embeds, given_embeds])
    mine, w_query, w_key, w_value, cache_keys, cache_values = lax.optimization_barrier(
        (mine, w_query, w_key, w_value, cache_keys, cache_values)
    )
    w_parts = [w_query[:, j * HD : (j + 1) * HD] for j in range(q_cols // HD)] + [w_key, w_value]
    w_len = len(w_parts) * w_rows
    key_start = -(-w_len // ctx_rows) * ctx_rows
    value_start = key_start + ctx_rows
    used = value_start + ctx_rows
    total_blocks = -(-used // w_rows)
    lead = jnp.zeros((key_start - w_len, HD), w_query.dtype)
    tail = jnp.zeros((total_blocks * w_rows - used, HD), w_query.dtype)
    packed = jnp.concatenate(w_parts + [lead, cache_keys, cache_values, tail], axis=0)

    n_ylo = lax.axis_size("ylo")
    n_z = lax.axis_size("z")
    me_ylo = lax.axis_index("ylo")
    me_z = lax.axis_index("z")
    me_core = lax.axis_index("core")

    both = lax.all_gather(mine, "tp", axis=2, tiled=True)
    first_rows, given_rows = both[0], both[1]

    revised = jnp.where(accept[:, None] == 1, given_rows, first_rows)
    normed = normalize(jnp.concatenate([first_rows, revised], axis=0), norm_gain)
    normed5 = normed.reshape(normed.shape[0], n_ylo, n_z, 2, w_rows)
    normed5 = jnp.roll(normed5, -me_ylo, axis=1)
    normed5 = jnp.roll(normed5, -me_z, axis=2)
    normed5 = jnp.roll(normed5, -me_core, axis=3)
    line = jnp.stack([packed] + [shifted(packed, "ylo", n_ylo, k) for k in range(1, n_ylo)])
    arrived = [(0, line)]
    forward = line
    backward = line
    far = n_z // 2
    split = n_ylo // 2
    for step in range(1, far):
        forward = shifted(forward, "z", n_z, -1)
        backward = shifted(backward, "z", n_z, 1)
        arrived += [(-step, forward), (step, backward)]
    pair_index = lambda z, core: (z % n_z) * 2 + core
    to_partner_front = [(pair_index(z - 1, 1 - c), pair_index(z, c)) for z in range(n_z) for c in range(2)]
    to_partner_back = [(pair_index(z + 1, 1 - c), pair_index(z, c)) for z in range(n_z) for c in range(2)]
    far_own = jnp.concatenate(
        [shifted(forward[:split], "z", n_z, -1), shifted(backward[split:], "z", n_z, 1)], axis=0
    )
    far_other = jnp.concatenate(
        [
            lax.ppermute(forward[:split], ("z", "core"), to_partner_front),
            lax.ppermute(backward[split:], ("z", "core"), to_partner_back),
        ],
        axis=0,
    )
    normed5, far_own, far_other = lax.optimization_barrier((normed5, far_own, far_other))
    held = [(offset, 0, piece) for offset, piece in arrived]
    held += [(offset, 1, shifted(piece, "core", 2, 1)) for offset, piece in arrived]
    held += [(far, 0, far_own), (far, 1, far_other)]

    proj = None
    for offset, core, piece in held:
        part = jnp.einsum(
            "rki,kjid->rjd",
            normed5[:, :, offset % n_z, core, :],
            piece.reshape(n_ylo, total_blocks, w_rows, HD),
            preferred_element_type=jnp.float32,
        )
        proj = part if proj is None else proj + part
    queries = proj[:, : q_cols // HD, :].reshape(-1, q_cols) + b_query.astype(jnp.float32)
    key_proj = proj[:, q_cols // HD, :] + b_key.astype(jnp.float32)
    value_proj = proj[:, q_cols // HD + 1, :] + b_value.astype(jnp.float32)
    length = lengths[0]
    keep_row = block_keep[0]
    positions = length.astype(jnp.float32) + jnp.arange(block_rows, dtype=jnp.float32)
    q_rot = rotate(queries.reshape(2, block_rows, q_cols // HD, HD), positions).astype(jnp.bfloat16)
    k_rot = rotate(key_proj.reshape(2, block_rows, local_kv, HD), positions).astype(jnp.bfloat16)
    value_rows = value_proj.astype(jnp.bfloat16)

    blocks_all = keep_row.shape[0]
    cache_index = jnp.arange(blocks_all * ctx_rows, dtype=jnp.int32).reshape(n_ylo, n_z, 2, ctx_rows)
    kept = jnp.broadcast_to(keep_row.reshape(n_ylo, n_z, 2, 1), cache_index.shape) == 1
    visible = (cache_index < length) & kept
    bias4 = jnp.where(visible, 0.0, -jnp.inf).astype(jnp.float32)
    bias4 = jnp.roll(bias4, -me_ylo, axis=0)
    bias4 = jnp.roll(bias4, -me_z, axis=1)
    bias4 = jnp.roll(bias4, -me_core, axis=2)
    bias = jnp.concatenate([bias4[:, offset % n_z, core, :].reshape(1, -1) for offset, core, ignored in held], axis=1)
    cache_k = jnp.concatenate(
        [piece[:, key_start:value_start, :].reshape(-1, HD) for ignored, ignored2, piece in held], axis=0
    )
    cache_v = jnp.concatenate(
        [piece[:, value_start:used, :].reshape(-1, HD) for ignored, ignored2, piece in held], axis=0
    )
    attended = attend(
        q_rot.reshape(2, block_rows, q_cols),
        k_rot.reshape(2, block_rows, local_kv * HD),
        value_rows.reshape(2, block_rows, local_kv * HD),
        cache_k,
        cache_v,
        bias,
    )
    return (attended[0], attended[1])


def solution(mesh):
    blk_size, tp_size = mesh.devices.shape
    fine = Mesh(mesh.devices.reshape(4, blk_size // 8, 2, tp_size), ("ylo", "z", "core", "tp"))
    rows = ("ylo", "z", "core")
    return jax.shard_map(
        local,
        mesh=fine,
        in_specs=(
            P(rows, "tp"),
            P(rows, "tp"),
            P(rows),
            P(rows),
            P(rows, None),
            P(),
            P(rows, "tp"),
            P("tp"),
            P(rows, "tp"),
            P("tp"),
            P(rows, "tp"),
            P("tp"),
            P(rows, "tp"),
            P(rows, "tp"),
        ),
        out_specs=(P(rows, "tp"), P(rows, "tp")),
        check_vma=False,
    )
```

```python
import math

import jax
import jax.numpy as jnp
from jax import lax
from jax.experimental import pallas as pl
from jax.experimental.pallas import tpu as pltpu
from jax.sharding import Mesh
from jax.sharding import PartitionSpec as P

KVH = 8
HD = 128
HQ = 40
CB = 64


def rotate(vectors, positions):
    halfway = HD // 2
    frequency = 1000000.0 ** (-(jnp.arange(halfway, dtype=jnp.float32) * (2.0 / HD)))
    angles = positions[..., None] * frequency
    cosine = jnp.cos(angles)[..., None, :]
    sine_part = jnp.sin(angles)[..., None, :]
    front_part = vectors[..., :halfway]
    back_part = vectors[..., halfway:]
    return jnp.concatenate(
        [front_part * cosine - back_part * sine_part, back_part * cosine + front_part * sine_part],
        axis=-1,
    )


def normalize(rows_in, norm_gain):
    widened = rows_in.astype(jnp.float32)
    inverse = lax.rsqrt(jnp.mean(widened * widened, axis=-1, keepdims=True) + 1e-06)
    return (widened * inverse * norm_gain.astype(jnp.float32)).astype(jnp.bfloat16)


def attend_kernel(q_ref, ko_ref, vo_ref, kc_ref, vc_ref, bias_ref, out_ref):
    inv_root = 1.0 / math.sqrt(HD)
    contract = (((1,), (1,)), ((), ()))
    own_keys = ko_ref[...]
    own_values = vo_ref[...]
    cache_k = kc_ref[...]
    cache_v = vc_ref[...]
    bias = bias_ref[...]
    for head in range(q_ref.shape[1] // HD):
        lanes = slice(head * HD, (head + 1) * HD)
        q = q_ref[:, lanes]
        own = lax.dot_general(q, own_keys, contract, preferred_element_type=jnp.float32) * inv_root
        far = lax.dot_general(q, cache_k, contract, preferred_element_type=jnp.float32) * inv_root
        far = far + bias
        highest = jnp.maximum(jnp.max(own, axis=-1, keepdims=True), jnp.max(far, axis=-1, keepdims=True))
        own_w = jnp.exp(own - highest)
        far_w = jnp.exp(far - highest)
        totals = jnp.sum(own_w, axis=-1, keepdims=True) + jnp.sum(far_w, axis=-1, keepdims=True)
        mixture = jnp.dot(own_w.astype(jnp.bfloat16), own_values, preferred_element_type=jnp.float32)
        mixture = mixture + jnp.dot(far_w.astype(jnp.bfloat16), cache_v, preferred_element_type=jnp.float32)
        out_ref[:, lanes] = (mixture / totals).astype(out_ref.dtype)


def attend(q_rot, k_rot, value_rows, cache_k, cache_v, bias):
    passes, rows, width = q_rot.shape
    heads = width // HD
    ctx = cache_k.shape[0]
    return pl.pallas_call(
        attend_kernel,
        grid=(passes,),
        in_specs=[
            pl.BlockSpec((None, rows, width), lambda p: (p, 0, 0)),
            pl.BlockSpec((None, rows, HD), lambda p: (p, 0, 0)),
            pl.BlockSpec((None, rows, HD), lambda p: (p, 0, 0)),
            pl.BlockSpec((ctx, HD), lambda p: (0, 0)),
            pl.BlockSpec((ctx, HD), lambda p: (0, 0)),
            pl.BlockSpec((1, ctx), lambda p: (0, 0)),
        ],
        out_specs=pl.BlockSpec((None, rows, width), lambda p: (p, 0, 0)),
        out_shape=jax.ShapeDtypeStruct((passes, rows, width), jnp.bfloat16),
        cost_estimate=pl.CostEstimate(
            flops=4 * passes * heads * rows * (ctx + rows) * HD,
            transcendentals=passes * heads * rows * (ctx + rows),
            bytes_accessed=2 * (2 * ctx * HD + 4 * passes * rows * width),
        ),
    )(q_rot, k_rot, value_rows, cache_k, cache_v, bias)


def shifted(x, axis, size, shift):
    pairs = [(j, (j - shift) % size) for j in range(size)]
    return lax.ppermute(x, axis, pairs)


def local(
    embeds,
    given_embeds,
    accept,
    lengths,
    block_keep,
    norm_gain,
    w_query,
    b_query,
    w_key,
    b_key,
    w_value,
    b_value,
    cache_keys,
    cache_values,
):
    local_kv = w_key.shape[1] // HD
    block_rows = embeds.shape[0]
    ctx_rows = cache_keys.shape[0]
    q_cols = w_query.shape[1]
    w_rows = w_query.shape[0]

    mine = jnp.stack([embeds, given_embeds])
    mine, w_query, w_key, w_value, cache_keys, cache_values = lax.optimization_barrier(
        (mine, w_query, w_key, w_value, cache_keys, cache_values)
    )
    w_parts = [w_query[:, j * HD : (j + 1) * HD] for j in range(q_cols // HD)] + [w_key, w_value]
    w_len = len(w_parts) * w_rows
    key_start = -(-w_len // ctx_rows) * ctx_rows
    value_start = key_start + ctx_rows
    used = value_start + ctx_rows
    total_blocks = -(-used // w_rows)
    lead = jnp.zeros((key_start - w_len, HD), w_query.dtype)
    tail = jnp.zeros((total_blocks * w_rows - used, HD), w_query.dtype)
    q_blocks = jnp.transpose(w_query.reshape(w_rows, q_cols // HD, HD), (1, 0, 2)).reshape(-1, HD)
    packed = jnp.concatenate([q_blocks, w_key, w_value, lead, cache_keys, cache_values, tail], axis=0)

    n_ylo = lax.axis_size("ylo")
    n_z = lax.axis_size("z")
    me_ylo = lax.axis_index("ylo")
    me_z = lax.axis_index("z")
    me_core = lax.axis_index("core")

    both = lax.all_gather(mine, "tp", axis=2, tiled=True)
    first_rows, given_rows = both[0], both[1]

    revised = jnp.where(accept[:, None] == 1, given_rows, first_rows)
    normed = normalize(jnp.concatenate([first_rows, revised], axis=0), norm_gain)
    normed5 = normed.reshape(normed.shape[0], n_ylo, n_z, 2, w_rows)
    normed5 = jnp.roll(normed5, -me_ylo, axis=1)
    normed5 = jnp.roll(normed5, -me_z, axis=2)
    normed5 = jnp.roll(normed5, -me_core, axis=3)
    line = jnp.stack([packed] + [shifted(packed, "ylo", n_ylo, k) for k in range(1, n_ylo)])
    arrived = [(0, line)]
    forward = line
    backward = line
    far = n_z // 2
    split = n_ylo // 2
    for step in range(1, far):
        forward = shifted(forward, "z", n_z, -1)
        backward = shifted(backward, "z", n_z, 1)
        arrived += [(-step, forward), (step, backward)]
    pair_index = lambda z, core: (z % n_z) * 2 + core
    to_partner_front = [(pair_index(z - 1, 1 - c), pair_index(z, c)) for z in range(n_z) for c in range(2)]
    to_partner_back = [(pair_index(z + 1, 1 - c), pair_index(z, c)) for z in range(n_z) for c in range(2)]
    far_own = jnp.concatenate(
        [shifted(forward[:split], "z", n_z, -1), shifted(backward[split:], "z", n_z, 1)], axis=0
    )
    far_other = jnp.concatenate(
        [
            lax.ppermute(forward[:split], ("z", "core"), to_partner_front),
            lax.ppermute(backward[split:], ("z", "core"), to_partner_back),
        ],
        axis=0,
    )
    normed5, far_own, far_other = lax.optimization_barrier((normed5, far_own, far_other))
    held = [(offset, 0, piece) for offset, piece in arrived]
    held += [(offset, 1, shifted(piece, "core", 2, 1)) for offset, piece in arrived]
    held += [(far, 0, far_own), (far, 1, far_other)]

    proj = None
    for offset, core, piece in held:
        part = jnp.einsum(
            "rki,kjid->rjd",
            normed5[:, :, offset % n_z, core, :],
            piece.reshape(n_ylo, total_blocks, w_rows, HD),
            preferred_element_type=jnp.float32,
        )
        proj = part if proj is None else proj + part
    queries = proj[:, : q_cols // HD, :].reshape(-1, q_cols) + b_query.astype(jnp.float32)
    key_proj = proj[:, q_cols // HD, :] + b_key.astype(jnp.float32)
    value_proj = proj[:, q_cols // HD + 1, :] + b_value.astype(jnp.float32)
    length = lengths[0]
    keep_row = block_keep[0]
    positions = length.astype(jnp.float32) + jnp.arange(block_rows, dtype=jnp.float32)
    q_rot = rotate(queries.reshape(2, block_rows, q_cols // HD, HD), positions).astype(jnp.bfloat16)
    k_rot = rotate(key_proj.reshape(2, block_rows, local_kv, HD), positions).astype(jnp.bfloat16)
    value_rows = value_proj.astype(jnp.bfloat16)

    blocks_all = keep_row.shape[0]
    cache_index = jnp.arange(blocks_all * ctx_rows, dtype=jnp.int32).reshape(n_ylo, n_z, 2, ctx_rows)
    kept = jnp.broadcast_to(keep_row.reshape(n_ylo, n_z, 2, 1), cache_index.shape) == 1
    visible = (cache_index < length) & kept
    bias4 = jnp.where(visible, 0.0, -jnp.inf).astype(jnp.float32)
    bias4 = jnp.roll(bias4, -me_ylo, axis=0)
    bias4 = jnp.roll(bias4, -me_z, axis=1)
    bias4 = jnp.roll(bias4, -me_core, axis=2)
    bias = jnp.concatenate([bias4[:, offset % n_z, core, :].reshape(1, -1) for offset, core, ignored in held], axis=1)
    cache_k = jnp.concatenate(
        [piece[:, key_start:value_start, :].reshape(-1, HD) for ignored, ignored2, piece in held], axis=0
    )
    cache_v = jnp.concatenate(
        [piece[:, value_start:used, :].reshape(-1, HD) for ignored, ignored2, piece in held], axis=0
    )
    attended = attend(
        q_rot.reshape(2, block_rows, q_cols),
        k_rot.reshape(2, block_rows, local_kv * HD),
        value_rows.reshape(2, block_rows, local_kv * HD),
        cache_k,
        cache_v,
        bias,
    )
    return (attended[0], attended[1])


def solution(mesh):
    blk_size, tp_size = mesh.devices.shape
    fine = Mesh(mesh.devices.reshape(4, blk_size // 8, 2, tp_size), ("ylo", "z", "core", "tp"))
    rows = ("ylo", "z", "core")
    return jax.shard_map(
        local,
        mesh=fine,
        in_specs=(
            P(rows, "tp"),
            P(rows, "tp"),
            P(rows),
            P(rows),
            P(rows, None),
            P(),
            P(rows, "tp"),
            P("tp"),
            P(rows, "tp"),
            P("tp"),
            P(rows, "tp"),
            P("tp"),
            P(rows, "tp"),
            P(rows, "tp"),
        ),
        out_specs=(P(rows, "tp"), P(rows, "tp")),
        check_vma=False,
    )
```
